512 devices in a mesh: dp: 32 (over y, x), feat: 16 (over z, core).
Axes of the slice: x: 4, y: 8, z: 8, core: 2. Of those that a mesh axis runs over, the one named last changes fastest.
Arguments:
- tokens: bfloat16 [4096, 8192], P('dp', 'feat'), may hold values from -6 to 6
- targets: bfloat16 [8192, 8192], P('dp', 'feat'), may hold values from -6 to 6
- first_blocks: bfloat16 [128, 64, 256], P('feat'), may hold values from -0.75 to 0.75
- second_factor_blocks: bfloat16 [128, 256, 256], P('feat'), may hold values from -0.375 to 0.375
- down_blocks: bfloat16 [128, 256, 64], P('feat'), may hold values from -0.375 to 0.375
- first_tangent: bfloat16 [128, 64, 256], P('feat'), may hold values from -0.75 to 0.75
- second_factor_tangent: bfloat16 [128, 256, 256], P('feat'), may hold values from -0.375 to 0.375
- doc_lengths: int32 [32, 32], replicated, may hold values from 1 to 8, as said below
- doc_owners: int32 [32, 32], replicated, may hold values from 0 to 31, as said below
- pack_offsets: int32 [32, 32], replicated, may hold values from 0 to 248, as said below
Outputs:
- hess_first: float32 [128, 64, 256], P('feat', 'dp')
- hess_mixed: float32 [128, 256, 256], P('feat', 'dp')
The draws below stay inside these ranges and needn't reach their ends.
Inputs may be any that keep to these rules, and one draw needn't show every extreme that they name: `doc_lengths`: the 32 lengths of one loader sum to 128; the longest has exactly 8 rows. `doc_owners`: A loader sends exactly one document to each owner; some owner receives exactly 256 rows in all, and none more. `pack_offsets`: each owner's documents lie end to end from row 0 of its pack, in the order of their loaders.
All inputs are finite; a program needn't handle non-finite values.
Results may differ from the reference program's by a relative error of at most 0.0072.
Values may be sent and summed in bfloat16 or wider, within the bound.
No kernel may reach another device: no remote copies, remote signals or barrier semaphores. Data moves between devices by JAX's collectives and lax.ppermute only.
A program may use at most 64 MiB of HBM per device.

```python
import jax
import jax.numpy as jnp
from jax import lax

D = 8192
NB = 128
BS = 256
TOK_DEV = 128
IN_B = 64
CM = 2
DOCS_DEV = 32
MOST = 8
OWN_CAP = 256
TOKENS = 4096
N_DP = 32


def doc_tables(key):
    loaders = N_DP
    docs = DOCS_DEV
    longest = MOST
    rank_owner = jax.random.permutation(jax.random.fold_in(key, 11), loaders).astype(jnp.int32)
    rank_loader = jax.random.permutation(jax.random.fold_in(key, 12), loaders).astype(jnp.int32)
    columns = jnp.arange(docs, dtype=jnp.int32)
    circle = (rank_loader[:, None] + columns[None, :]) % loaders
    owners = rank_owner[circle]
    long_col = (loaders - rank_loader) % loaders
    is_long = columns[None, :] == long_col[:, None]
    shares = jax.random.randint(jax.random.fold_in(key, 14), (loaders, docs), 4, 8, dtype=jnp.int32)
    shares = jnp.where(is_long, 0, shares)
    extra = TOK_DEV - longest - (docs - 1)
    share_total = jnp.sum(shares, axis=1, keepdims=True)
    portion = extra * shares // share_total
    leftover = extra - jnp.sum(portion, axis=1, keepdims=True)
    order_rank = jnp.cumsum(jnp.logical_not(is_long).astype(jnp.int32), axis=1) - 1
    lengths = jnp.where(is_long, longest, 1 + portion + (order_rank < leftover).astype(jnp.int32))
    matched = (owners[:, :, None] == jnp.arange(loaders, dtype=jnp.int32)[None, None, :]).astype(jnp.int32)
    owner_load = jnp.sum(matched * lengths[:, :, None], axis=1)
    before = jnp.cumsum(owner_load, axis=0) - owner_load
    offsets = jnp.sum(matched * before[:, None, :], axis=2)
    return (lengths.astype(jnp.int32), owners.astype(jnp.int32), offsets.astype(jnp.int32))


def draw_doc_lengths(key, part):
    return doc_tables(key)[0]


def draw_doc_owners(key, part):
    return doc_tables(key)[1]


def draw_pack_offsets(key, part):
    return doc_tables(key)[2]


def level_of(key, shape, pieces, least, high):
    def one(dim, blocks):
        draws = jax.random.uniform(jax.random.fold_in(jax.random.fold_in(key, 6), dim), (blocks,), jnp.float32, least / len(pieces), high / len(pieces))
        return jnp.repeat(jnp.exp(draws), shape[dim] // blocks).reshape((-1,) + (1,) * (len(shape) - dim - 1))

    factor_of = one(*pieces[0])
    for cut in pieces[1:]:
        factor_of = factor_of * one(*cut)
    return factor_of


def noise(stream_key, dims, scale, bound, shards=(), kind=jnp.bfloat16):
    gain = level_of(stream_key, dims, shards, -0.22, 0.18) if shards else 1.0
    array = jax.random.normal(stream_key, dims, jnp.float32) * scale * gain
    return jnp.minimum(jnp.maximum(array, -bound), bound).astype(kind)


def setup_inputs(seed: int = 0) -> dict:
    streams_of = jax.random.split(jax.random.key(seed), 11)
    return {
        "tokens": noise(streams_of[0], (TOKENS, D), 1.0, 6.0, ((0, 32), (1, 16))),
        "targets": noise(streams_of[1], (N_DP * OWN_CAP, D), 1.0, 6.0, ((0, 32), (1, 16))),
        "first_blocks": noise(streams_of[2], (NB, D // NB, BS), (D // NB) ** -0.5, 0.75, ((0, 16),)),
        "second_factor_blocks": noise(streams_of[3], (NB, BS, BS), BS ** -0.5, 0.375, ((0, 16),)),
        "down_blocks": noise(streams_of[4], (NB, BS, D // NB), BS ** -0.5, 0.375, ((0, 16),)),
        "first_tangent": noise(streams_of[5], (NB, D // NB, BS), (D // NB) ** -0.5, 0.75, ((0, 16),)),
        "second_factor_tangent": noise(streams_of[6], (NB, BS, BS), BS ** -0.5, 0.375, ((0, 16),)),
        "doc_lengths": draw_doc_lengths(jax.random.fold_in(streams_of[10], 71), 0),
        "doc_owners": draw_doc_owners(jax.random.fold_in(streams_of[10], 71), 0),
        "pack_offsets": draw_pack_offsets(jax.random.fold_in(streams_of[10], 71), 0),
    }


inv_root_two = 0.7071067811865476
inv_root_two_pi = 0.3989422804014327


def permute_blocks(values):
    row_count = values.shape[0]
    return values.reshape(row_count, NB, NB, CM).transpose(0, 2, 1, 3).reshape(row_count, NB, BS)


def round_wide(values):
    return lax.optimization_barrier(values.astype(jnp.bfloat16)).astype(jnp.float32)


def reference(tokens, targets, first_blocks, second_factor_blocks, down_blocks, first_tangent, second_factor_tangent, doc_lengths, doc_owners, pack_offsets):
    first_full = first_blocks.astype(jnp.float32)
    mixed_full = second_factor_blocks.astype(jnp.float32)
    down_full = down_blocks.astype(jnp.float32)
    first_tan_full = first_tangent.astype(jnp.float32)
    mixed_tan_full = second_factor_tangent.astype(jnp.float32)
    position = jnp.arange(TOK_DEV, dtype=jnp.int32)

    def one_loader(carry, loader):
        hess_first, hess_mixed = carry
        tok_rows = lax.dynamic_slice_in_dim(tokens, loader * TOK_DEV, TOK_DEV, 0)
        lengths = doc_lengths[loader]
        owners = doc_owners[loader]
        offsets = pack_offsets[loader]
        starts = jnp.cumsum(lengths) - lengths
        inside = (position[:, None] >= starts[None, :]) & (position[:, None] < (starts + lengths)[None, :])
        inside_int = inside.astype(jnp.int32)
        goal_index = jnp.sum(inside_int * (owners * OWN_CAP + offsets - starts)[None, :], axis=1) + position
        weight = jnp.sum(inside.astype(jnp.float32) / lengths.astype(jnp.float32)[None, :], axis=1)
        goal_rows = jnp.take(targets, goal_index.astype(jnp.int32), axis=0)
        token_blocks = tok_rows.astype(jnp.float32).reshape(TOK_DEV, NB, IN_B)
        goal_blocks = goal_rows.astype(jnp.float32).reshape(TOK_DEV, NB, IN_B)
        first_act = round_wide(jnp.einsum("tki,kij->tkj", token_blocks, first_full))
        tan_act = round_wide(jnp.einsum("tki,kij->tkj", token_blocks, first_tan_full))
        out_grad = round_wide(jnp.einsum("tkd,kmd->tkm", goal_blocks, down_full) * weight[:, None, None])
        mixed_activation = permute_blocks(first_act)
        mixed_tangent_value = permute_blocks(tan_act)
        hidden_grad = permute_blocks(out_grad)
        pre_act = jnp.einsum("tgm,gmj->tgj", mixed_activation, mixed_full)
        pre_tan = jnp.einsum("tgm,gmj->tgj", mixed_tangent_value, mixed_full) + jnp.einsum("tgm,gmj->tgj", mixed_activation, mixed_tan_full)
        density = jnp.exp(-0.5 * pre_act * pre_act) * inv_root_two_pi
        normal_cdf = 0.5 * (1.0 + lax.erf(pre_act * inv_root_two))
        preactivation_gradient = round_wide(hidden_grad * (normal_cdf + pre_act * density))
        preactivation_tangent_gradient = round_wide(hidden_grad * (density * (2.0 - pre_act * pre_act)) * pre_tan)
        hess_mixed = hess_mixed + jnp.einsum("tgm,tgj->gmj", mixed_tangent_value, preactivation_gradient) + jnp.einsum("tgm,tgj->gmj", mixed_activation, preactivation_tangent_gradient)
        back_mixed = round_wide(jnp.einsum("tgj,gmj->tgm", preactivation_tangent_gradient, mixed_full) + jnp.einsum("tgj,gmj->tgm", preactivation_gradient, mixed_tan_full))
        back_first = permute_blocks(back_mixed)
        hess_first = hess_first + jnp.einsum("tki,tkj->kij", token_blocks, back_first)
        return (hess_first, hess_mixed), None

    first_factor_start = jnp.zeros((NB, IN_B, BS), jnp.float32)
    start_mixed = jnp.zeros((NB, BS, BS), jnp.float32)
    (hess_first, hess_mixed), _ = lax.scan(one_loader, (first_factor_start, start_mixed), jnp.arange(N_DP, dtype=jnp.int32))
    return hess_first, hess_mixed
```

```python
import jax
import jax.numpy as jnp
from jax import lax
from jax.sharding import PartitionSpec as P

inv_root_two = 0.7071067811865476
inv_root_two_pi = 0.3989422804014327


def curvature(
    tok_rows,
    goal_rows,
    weight,
    first_blocks,
    second_factor_blocks,
    down_blocks,
    first_tangent,
    second_factor_tangent,
):
    features = lax.axis_size("feat")
    row_count = tok_rows.shape[0]
    local_blocks, block_in, block_out = first_blocks.shape
    pair_size = block_out // (local_blocks * features)
    token_blocks = tok_rows.reshape(row_count, local_blocks, block_in)
    goal_blocks = goal_rows.reshape(row_count, local_blocks, block_in)
    split_shape = (local_blocks, block_in, features, local_blocks, pair_size)
    down_shape = (local_blocks, features, local_blocks, pair_size, block_in)
    first_act = jnp.einsum(
        "rki,kiGgc->Ggkcr",
        token_blocks,
        first_blocks.reshape(split_shape),
        preferred_element_type=jnp.float32,
    ).astype(jnp.bfloat16)
    tangents = jnp.einsum(
        "rki,kiGgc->Ggkcr",
        token_blocks,
        first_tangent.reshape(split_shape),
        preferred_element_type=jnp.float32,
    ).astype(jnp.bfloat16)
    out_grad = (
        jnp.einsum(
            "rkd,kGgcd->Ggkcr",
            goal_blocks,
            down_blocks.reshape(down_shape),
            preferred_element_type=jnp.float32,
        )
        * weight
    ).astype(jnp.bfloat16)
    stacked = jnp.stack([first_act, tangents, out_grad], axis=1)
    mixed = lax.all_to_all(stacked, "feat", split_axis=0, concat_axis=3, tiled=True)
    hidden_shape = (local_blocks, block_out, row_count)
    mixed_activation = mixed[0, 0].reshape(hidden_shape)
    mixed_tangent_value = mixed[0, 1].reshape(hidden_shape)
    hidden_grad = mixed[0, 2].reshape(hidden_shape)
    pre_act = jnp.einsum(
        "vca,vcf->vfa", mixed_activation, second_factor_blocks, preferred_element_type=jnp.float32
    )
    pre_tan = jnp.einsum(
        "vca,vcf->vfa",
        mixed_tangent_value,
        second_factor_blocks,
        preferred_element_type=jnp.float32,
    ) + jnp.einsum(
        "vca,vcf->vfa", mixed_activation, second_factor_tangent, preferred_element_type=jnp.float32
    )
    density = jnp.exp(-0.5 * pre_act * pre_act) * inv_root_two_pi
    normal_cdf = 0.5 * (1.0 + lax.erf(pre_act * inv_root_two))
    preactivation_gradient = (hidden_grad * (normal_cdf + pre_act * density)).astype(jnp.bfloat16)
    preactivation_tangent_gradient = (
        hidden_grad * (density * (2.0 - pre_act * pre_act)) * pre_tan
    ).astype(jnp.bfloat16)
    hess_mixed = jnp.einsum(
        "evp,eqp->evq",
        mixed_tangent_value,
        preactivation_gradient,
        preferred_element_type=jnp.float32,
    ) + jnp.einsum(
        "evp,eqp->evq",
        mixed_activation,
        preactivation_tangent_gradient,
        preferred_element_type=jnp.float32,
    )
    back_mixed = jnp.einsum(
        "bip,bfi->bfp",
        preactivation_tangent_gradient,
        second_factor_blocks,
        preferred_element_type=jnp.float32,
    ) + jnp.einsum(
        "bip,bfi->bfp",
        preactivation_gradient,
        second_factor_tangent,
        preferred_element_type=jnp.float32,
    )
    back_split = back_mixed.astype(jnp.bfloat16).reshape(
        local_blocks, features, local_blocks, pair_size, row_count
    )
    back_first = lax.all_to_all(back_split, "feat", split_axis=1, concat_axis=0, tiled=True)
    back_first = back_first.reshape(local_blocks * features, local_blocks, pair_size, row_count)
    hess_first = jnp.einsum(
        "gkcr,rki->kigc", back_first, token_blocks, preferred_element_type=jnp.float32
    ).reshape(local_blocks, block_in, block_out)
    return (hess_first, hess_mixed)


def per_device(
    tokens,
    targets,
    first_blocks,
    second_factor_blocks,
    down_blocks,
    first_tangent,
    second_factor_tangent,
    doc_lengths,
    doc_owners,
    pack_offsets,
):
    loaders = lax.axis_size("dp")
    device = lax.axis_index("dp")
    tok_count = tokens.shape[0]
    feature_cols = tokens.shape[1]
    slot_rows = 2 * tok_count // loaders
    position = jnp.arange(slot_rows, dtype=jnp.int32)
    mine = (doc_owners == device).astype(jnp.int32)
    first_row = jnp.sum(mine * pack_offsets, axis=1)
    doc_span = jnp.sum(mine * doc_lengths, axis=1)
    in_slot = position[None, :] < doc_span[:, None]
    source = jnp.where(in_slot, first_row[:, None] + position[None, :], 0)
    outgoing = jnp.take(targets, source.reshape(-1), axis=0).reshape(
        loaders, slot_rows, feature_cols
    )
    arrived = lax.all_to_all(outgoing, "dp", split_axis=0, concat_axis=0, tiled=True)
    my_lengths = lax.dynamic_index_in_dim(doc_lengths, device, 0, keepdims=False)
    my_owners = lax.dynamic_index_in_dim(doc_owners, device, 0, keepdims=False)
    my_starts = jnp.cumsum(my_lengths) - my_lengths
    token_pos = jnp.arange(tok_count, dtype=jnp.int32)
    inside = (token_pos[:, None] >= my_starts[None, :]) & (
        token_pos[:, None] < (my_starts + my_lengths)[None, :]
    )
    inside_int = inside.astype(jnp.int32)
    goal_index = (
        jnp.sum(inside_int * (my_owners * slot_rows - my_starts)[None, :], axis=1) + token_pos
    )
    weight = jnp.sum(
        inside.astype(jnp.float32) / my_lengths.astype(jnp.float32)[None, :], axis=1
    )
    goal_rows = jnp.take(
        arrived.reshape(loaders * slot_rows, feature_cols), goal_index, axis=0
    )
    hess_first, hess_mixed = curvature(
        tokens,
        goal_rows,
        weight,
        first_blocks,
        second_factor_blocks,
        down_blocks,
        first_tangent,
        second_factor_tangent,
    )
    local_blocks = hess_first.shape[0]
    first_part = hess_first.reshape(local_blocks, loaders, -1)
    mixed_part = hess_mixed.reshape(local_blocks, loaders, -1)
    first_width = first_part.shape[2]
    partials = jnp.concatenate([first_part, mixed_part], axis=2)
    gathered = lax.all_to_all(partials, "dp", split_axis=1, concat_axis=1, tiled=True)
    total = jnp.sum(gathered, axis=1)
    hess_first = total[:, :first_width].reshape(local_blocks, -1, hess_first.shape[2])
    hess_mixed = total[:, first_width:].reshape(local_blocks, -1, hess_mixed.shape[2])
    return (hess_first, hess_mixed)


def solution(mesh):
    in_specs = (
        P("dp", "feat"),
        P("dp", "feat"),
        P("feat", None, None),
        P("feat", None, None),
        P("feat", None, None),
        P("feat", None, None),
        P("feat", None, None),
        P(),
        P(),
        P(),
    )
    out_specs = (P("feat", "dp", None), P("feat", "dp", None))
    return jax.shard_map(
        per_device, mesh=mesh, in_specs=in_specs, out_specs=out_specs, check_vma=False
    )
```

```python
import jax
import jax.numpy as jnp
from jax import lax
from jax.sharding import PartitionSpec as P

inv_root_two = 0.7071067811865476
inv_root_two_pi = 0.3989422804014327


def curvature(
    tok_rows,
    goal_rows,
    weight,
    first_blocks,
    second_factor_blocks,
    down_blocks,
    first_tangent,
    second_factor_tangent,
):
    features = lax.axis_size("feat")
    row_count = tok_rows.shape[0]
    local_blocks, block_in, block_out = first_blocks.shape
    pair_size = block_out // (local_blocks * features)
    token_blocks = tok_rows.reshape(row_count, local_blocks, block_in)
    goal_blocks = goal_rows.reshape(row_count, local_blocks, block_in)
    split_shape = (local_blocks, block_in, features, local_blocks, pair_size)
    down_shape = (local_blocks, features, local_blocks, pair_size, block_in)
    first_act = jnp.einsum(
        "rki,kiGgc->Ggkcr",
        token_blocks,
        first_blocks.reshape(split_shape),
        preferred_element_type=jnp.float32,
    ).astype(jnp.bfloat16)
    tangents = jnp.einsum(
        "rki,kiGgc->Ggkcr",
        token_blocks,
        first_tangent.reshape(split_shape),
        preferred_element_type=jnp.float32,
    ).astype(jnp.bfloat16)
    out_grad = (
        jnp.einsum(
            "rkd,kGgcd->Ggkcr",
            goal_blocks,
            down_blocks.reshape(down_shape),
            preferred_element_type=jnp.float32,
        )
        * weight
    ).astype(jnp.bfloat16)
    merged = (features, local_blocks, local_blocks * pair_size, row_count)
    stacked = jnp.stack(
        [first_act.reshape(merged), tangents.reshape(merged), out_grad.reshape(merged)], axis=1
    )
    mixed = lax.all_to_all(stacked, "feat", split_axis=0, concat_axis=3, tiled=True)
    hidden_shape = (local_blocks, block_out, row_count)
    mixed_activation = mixed[0, 0].reshape(hidden_shape)
    mixed_tangent_value = mixed[0, 1].reshape(hidden_shape)
    hidden_grad = mixed[0, 2].reshape(hidden_shape)
    pre_act = jnp.einsum(
        "vca,vcf->vfa", mixed_activation, second_factor_blocks, preferred_element_type=jnp.float32
    )
    pre_tan = jnp.einsum(
        "vca,vcf->vfa",
        mixed_tangent_value,
        second_factor_blocks,
        preferred_element_type=jnp.float32,
    ) + jnp.einsum(
        "vca,vcf->vfa", mixed_activation, second_factor_tangent, preferred_element_type=jnp.float32
    )
    density = jnp.exp(-0.5 * pre_act * pre_act) * inv_root_two_pi
    normal_cdf = 0.5 * (1.0 + lax.erf(pre_act * inv_root_two))
    preactivation_gradient = (hidden_grad * (normal_cdf + pre_act * density)).astype(jnp.bfloat16)
    preactivation_tangent_gradient = (
        hidden_grad * (density * (2.0 - pre_act * pre_act)) * pre_tan
    ).astype(jnp.bfloat16)
    loaders = lax.axis_size("dp")
    mixed_tan_split = mixed_tangent_value.reshape(local_blocks, loaders, -1, row_count)
    mixed_act_split = mixed_activation.reshape(local_blocks, loaders, -1, row_count)
    hess_mixed = jnp.einsum(
        "eDvp,eqp->Devq",
        mixed_tan_split,
        preactivation_gradient,
        preferred_element_type=jnp.float32,
    ) + jnp.einsum(
        "eDvp,eqp->Devq",
        mixed_act_split,
        preactivation_tangent_gradient,
        preferred_element_type=jnp.float32,
    )
    pos_shape = (local_blocks, features, local_blocks, pair_size, block_out)
    back_mixed = jnp.einsum(
        "bip,bFkci->Fkbcp",
        preactivation_tangent_gradient,
        second_factor_blocks.reshape(pos_shape),
        preferred_element_type=jnp.float32,
    ) + jnp.einsum(
        "bip,bFkci->Fkbcp",
        preactivation_gradient,
        second_factor_tangent.reshape(pos_shape),
        preferred_element_type=jnp.float32,
    )
    back_merged = back_mixed.astype(jnp.bfloat16).reshape(
        features, local_blocks, local_blocks * pair_size, row_count
    )
    back_first = lax.all_to_all(back_merged, "feat", split_axis=0, concat_axis=2, tiled=True)
    back_first = back_first.reshape(local_blocks, block_out, row_count)
    hess_first = jnp.einsum(
        "rki,kjr->kij", token_blocks, back_first, preferred_element_type=jnp.float32
    )
    return (hess_first, hess_mixed)


def per_device(
    tokens,
    targets,
    first_blocks,
    second_factor_blocks,
    down_blocks,
    first_tangent,
    second_factor_tangent,
    doc_lengths,
    doc_owners,
    pack_offsets,
):
    loaders = lax.axis_size("dp")
    device = lax.axis_index("dp")
    tok_count = tokens.shape[0]
    feature_cols = tokens.shape[1]
    slot_rows = 2 * tok_count // loaders
    position = jnp.arange(slot_rows, dtype=jnp.int32)
    mine = (doc_owners == device).astype(jnp.int32)
    first_row = jnp.sum(mine * pack_offsets, axis=1)
    doc_span = jnp.sum(mine * doc_lengths, axis=1)
    in_slot = position[None, :] < doc_span[:, None]
    source = jnp.where(in_slot, first_row[:, None] + position[None, :], 0)
    outgoing = jnp.take(targets, source.reshape(-1), axis=0).reshape(
        loaders, slot_rows, feature_cols
    )
    arrived = lax.all_to_all(outgoing, "dp", split_axis=0, concat_axis=0, tiled=True)
    my_lengths = lax.dynamic_index_in_dim(doc_lengths, device, 0, keepdims=False)
    my_owners = lax.dynamic_index_in_dim(doc_owners, device, 0, keepdims=False)
    my_starts = jnp.cumsum(my_lengths) - my_lengths
    token_pos = jnp.arange(tok_count, dtype=jnp.int32)
    inside = (token_pos[:, None] >= my_starts[None, :]) & (
        token_pos[:, None] < (my_starts + my_lengths)[None, :]
    )
    inside_int = inside.astype(jnp.int32)
    goal_index = (
        jnp.sum(inside_int * (my_owners * slot_rows - my_starts)[None, :], axis=1) + token_pos
    )
    weight = jnp.sum(
        inside.astype(jnp.float32) / my_lengths.astype(jnp.float32)[None, :], axis=1
    )
    goal_rows = jnp.take(
        arrived.reshape(loaders * slot_rows, feature_cols), goal_index, axis=0
    )
    hess_first, hess_mixed = curvature(
        tokens,
        goal_rows,
        weight,
        first_blocks,
        second_factor_blocks,
        down_blocks,
        first_tangent,
        second_factor_tangent,
    )
    local_blocks = hess_first.shape[0]
    first_part = hess_first.reshape(local_blocks, loaders, -1).transpose(1, 0, 2)
    mixed_part = hess_mixed.reshape(loaders, local_blocks, -1)
    first_width = first_part.shape[2]
    partials = jnp.concatenate([first_part, mixed_part], axis=2).astype(jnp.bfloat16)
    gathered = lax.all_to_all(partials, "dp", split_axis=0, concat_axis=0, tiled=True)
    total = jnp.sum(gathered.astype(jnp.float32), axis=0)
    hess_first = total[:, :first_width].reshape(local_blocks, -1, first_blocks.shape[2])
    hess_mixed = total[:, first_width:].reshape(local_blocks, -1, second_factor_blocks.shape[2])
    return (hess_first, hess_mixed)


def solution(mesh):
    in_specs = (
        P("dp", "feat"),
        P("dp", "feat"),
        P("feat", None, None),
        P("feat", None, None),
        P("feat", None, None),
        P("feat", None, None),
        P("feat", None, None),
        P(),
        P(),
        P(),
    )
    out_specs = (P("feat", "dp", None), P("feat", "dp", None))
    return jax.shard_map(
        per_device, mesh=mesh, in_specs=in_specs, out_specs=out_specs, check_vma=False
    )
```

```python
import jax
import jax.numpy as jnp
from jax import lax
from jax.sharding import PartitionSpec as P

inv_root_two = 0.7071067811865476
inv_root_two_pi = 0.3989422804014327


def curvature(
    tok_rows,
    goal_rows,
    weight,
    first_blocks,
    second_factor_blocks,
    down_blocks,
    first_tangent,
    second_factor_tangent,
):
    features = lax.axis_size("feat")
    row_count = tok_rows.shape[0]
    local_blocks, block_in, block_out = first_blocks.shape
    pair_size = block_out // (local_blocks * features)
    token_blocks = tok_rows.reshape(row_count, local_blocks, block_in)
    goal_blocks = goal_rows.reshape(row_count, local_blocks, block_in)
    split_shape = (local_blocks, block_in, features, local_blocks, pair_size)
    down_shape = (local_blocks, features, local_blocks, pair_size, block_in)
    first_act = jnp.einsum(
        "rki,kiGgc->Ggkcr",
        token_blocks,
        first_blocks.reshape(split_shape),
        preferred_element_type=jnp.float32,
    ).astype(jnp.bfloat16)
    tangents = jnp.einsum(
        "rki,kiGgc->Ggkcr",
        token_blocks,
        first_tangent.reshape(split_shape),
        preferred_element_type=jnp.float32,
    ).astype(jnp.bfloat16)
    out_grad = (
        jnp.einsum(
            "rkd,kGgcd->Ggkcr",
            goal_blocks,
            down_blocks.reshape(down_shape),
            preferred_element_type=jnp.float32,
        )
        * weight
    ).astype(jnp.bfloat16)
    merged = (features, local_blocks, local_blocks * pair_size, row_count)
    stacked = jnp.stack(
        [first_act.reshape(merged), tangents.reshape(merged), out_grad.reshape(merged)], axis=1
    )
    mixed = lax.all_to_all(stacked, "feat", split_axis=0, concat_axis=3, tiled=True)
    hidden_shape = (local_blocks, block_out, row_count)
    mixed_activation = mixed[0, 0].reshape(hidden_shape)
    mixed_tangent_value = mixed[0, 1].reshape(hidden_shape)
    hidden_grad = mixed[0, 2].reshape(hidden_shape)
    pre_act = jnp.einsum(
        "vca,vcf->vfa", mixed_activation, second_factor_blocks, preferred_element_type=jnp.float32
    )
    pre_tan = jnp.einsum(
        "vca,vcf->vfa",
        mixed_tangent_value,
        second_factor_blocks,
        preferred_element_type=jnp.float32,
    ) + jnp.einsum(
        "vca,vcf->vfa", mixed_activation, second_factor_tangent, preferred_element_type=jnp.float32
    )
    density = jnp.exp(-0.5 * pre_act * pre_act) * inv_root_two_pi
    normal_cdf = 0.5 * (1.0 + lax.erf(pre_act * inv_root_two))
    preactivation_gradient = (hidden_grad * (normal_cdf + pre_act * density)).astype(jnp.bfloat16)
    preactivation_tangent_gradient = (
        hidden_grad * (density * (2.0 - pre_act * pre_act)) * pre_tan
    ).astype(jnp.bfloat16)
    hess_mixed = jnp.einsum(
        "evp,eqp->evq",
        mixed_tangent_value,
        preactivation_gradient,
        preferred_element_type=jnp.float32,
    ) + jnp.einsum(
        "evp,eqp->evq",
        mixed_activation,
        preactivation_tangent_gradient,
        preferred_element_type=jnp.float32,
    )
    pos_shape = (local_blocks, features, local_blocks, pair_size, block_out)
    back_mixed = jnp.einsum(
        "bip,bFkci->Fkbcp",
        preactivation_tangent_gradient,
        second_factor_blocks.reshape(pos_shape),
        preferred_element_type=jnp.float32,
    ) + jnp.einsum(
        "bip,bFkci->Fkbcp",
        preactivation_gradient,
        second_factor_tangent.reshape(pos_shape),
        preferred_element_type=jnp.float32,
    )
    back_merged = back_mixed.astype(jnp.bfloat16).reshape(
        features, local_blocks, local_blocks * pair_size, row_count
    )
    back_first = lax.all_to_all(back_merged, "feat", split_axis=0, concat_axis=2, tiled=True)
    back_first = back_first.reshape(local_blocks, block_out, row_count)
    hess_first = jnp.einsum(
        "rki,kjr->kij", token_blocks, back_first, preferred_element_type=jnp.float32
    )
    return (hess_first, hess_mixed)


def per_device(
    tokens,
    targets,
    first_blocks,
    second_factor_blocks,
    down_blocks,
    first_tangent,
    second_factor_tangent,
    doc_lengths,
    doc_owners,
    pack_offsets,
):
    loaders = lax.axis_size("dp")
    device = lax.axis_index("dp")
    tok_count = tokens.shape[0]
    feature_cols = tokens.shape[1]
    slot_rows = 2 * tok_count // loaders
    position = jnp.arange(slot_rows, dtype=jnp.int32)
    mine = (doc_owners == device).astype(jnp.int32)
    first_row = jnp.sum(mine * pack_offsets, axis=1)
    doc_span = jnp.sum(mine * doc_lengths, axis=1)
    in_slot = position[None, :] < doc_span[:, None]
    source = jnp.where(in_slot, first_row[:, None] + position[None, :], 0)
    outgoing = jnp.take(targets, source.reshape(-1), axis=0).reshape(
        loaders, slot_rows, feature_cols
    )
    arrived = lax.all_to_all(outgoing, "dp", split_axis=0, concat_axis=0, tiled=True)
    my_lengths = lax.dynamic_index_in_dim(doc_lengths, device, 0, keepdims=False)
    my_owners = lax.dynamic_index_in_dim(doc_owners, device, 0, keepdims=False)
    my_starts = jnp.cumsum(my_lengths) - my_lengths
    token_pos = jnp.arange(tok_count, dtype=jnp.int32)
    inside = (token_pos[:, None] >= my_starts[None, :]) & (
        token_pos[:, None] < (my_starts + my_lengths)[None, :]
    )
    inside_int = inside.astype(jnp.int32)
    goal_index = (
        jnp.sum(inside_int * (my_owners * slot_rows - my_starts)[None, :], axis=1) + token_pos
    )
    weight = jnp.sum(
        inside.astype(jnp.float32) / my_lengths.astype(jnp.float32)[None, :], axis=1
    )
    goal_rows = jnp.take(
        arrived.reshape(loaders * slot_rows, feature_cols), goal_index, axis=0
    )
    hess_first, hess_mixed = curvature(
        tokens,
        goal_rows,
        weight,
        first_blocks,
        second_factor_blocks,
        down_blocks,
        first_tangent,
        second_factor_tangent,
    )
    local_blocks = hess_first.shape[0]
    first_part = hess_first.reshape(local_blocks, loaders, -1).transpose(1, 0, 2)
    mixed_part = hess_mixed.reshape(local_blocks, loaders, -1).transpose(1, 0, 2)
    first_width = first_part.shape[2]
    partials = jnp.concatenate([first_part, mixed_part], axis=2).astype(jnp.bfloat16)
    gathered = lax.all_to_all(partials, "dp", split_axis=0, concat_axis=0, tiled=True)
    total = jnp.sum(gathered.astype(jnp.float32), axis=0)
    hess_first = total[:, :first_width].reshape(local_blocks, -1, first_blocks.shape[2])
    hess_mixed = total[:, first_width:].reshape(local_blocks, -1, second_factor_blocks.shape[2])
    return (hess_first, hess_mixed)


def solution(mesh):
    in_specs = (
        P("dp", "feat"),
        P("dp", "feat"),
        P("feat", None, None),
        P("feat", None, None),
        P("feat", None, None),
        P("feat", None, None),
        P("feat", None, None),
        P(),
        P(),
        P(),
    )
    out_specs = (P("feat", "dp", None), P("feat", "dp", None))
    return jax.shard_map(
        per_device, mesh=mesh, in_specs=in_specs, out_specs=out_specs, check_vma=False
    )
```

```python
import jax
import jax.numpy as jnp
from jax import lax
from jax.experimental import pallas as pl
from jax.sharding import PartitionSpec as P

inv_root_two = 0.7071067811865476
inv_root_two_pi = 0.3989422804014327


def second_factor_kernel(recv_ref, w_t_ref, wt_t_ref, w_ref, wt_ref, back_ref, hess_ref):
    units = recv_ref.shape[0] * recv_ref.shape[3]
    rows = recv_ref.shape[4]
    mixed_activation = recv_ref[:, 0, 0].reshape(units, rows)
    mixed_tangent_value = recv_ref[:, 1, 0].reshape(units, rows)
    hidden_grad = recv_ref[:, 2, 0].reshape(units, rows).astype(jnp.float32)
    w_t = w_t_ref[0]
    pre_act = jnp.dot(w_t, mixed_activation, preferred_element_type=jnp.float32)
    pre_tan = jnp.dot(w_t, mixed_tangent_value, preferred_element_type=jnp.float32) + jnp.dot(
        wt_t_ref[0], mixed_activation, preferred_element_type=jnp.float32
    )
    density = jnp.exp(-0.5 * pre_act * pre_act) * inv_root_two_pi
    normal_cdf = 0.5 * (1.0 + lax.erf(pre_act * inv_root_two))
    preactivation_gradient = (hidden_grad * (normal_cdf + pre_act * density)).astype(jnp.bfloat16)
    preactivation_tangent_gradient = (
        hidden_grad * (density * (2.0 - pre_act * pre_act)) * pre_tan
    ).astype(jnp.bfloat16)
    back = jnp.dot(
        w_ref[0], preactivation_tangent_gradient, preferred_element_type=jnp.float32
    ) + jnp.dot(wt_ref[0], preactivation_gradient, preferred_element_type=jnp.float32)
    back_ref[0] = back.astype(jnp.bfloat16)
    row_contract = (((1,), (1,)), ((), ()))
    hess = lax.dot_general(
        mixed_tangent_value, preactivation_gradient, row_contract, preferred_element_type=jnp.float32
    ) + lax.dot_general(
        mixed_activation, preactivation_tangent_gradient, row_contract, preferred_element_type=jnp.float32
    )
    hess_ref[0] = hess.astype(jnp.bfloat16)


def second_factor(received, second_factor_blocks, second_factor_tangent):
    sources, kinds, local_blocks, pieces, rows = received.shape
    units = second_factor_blocks.shape[1]
    out_units = second_factor_blocks.shape[2]
    recv_spec = pl.BlockSpec((sources, kinds, 1, pieces, rows), lambda g: (0, 0, g, 0, 0))
    weight_spec = pl.BlockSpec((1, units, out_units), lambda g: (g, 0, 0))
    return pl.pallas_call(
        second_factor_kernel,
        grid=(local_blocks,),
        in_specs=[recv_spec, weight_spec, weight_spec, weight_spec, weight_spec],
        out_specs=[
            pl.BlockSpec((1, units, rows), lambda g: (g, 0, 0)),
            pl.BlockSpec((1, units, out_units), lambda g: (g, 0, 0)),
        ],
        out_shape=[
            jax.ShapeDtypeStruct((local_blocks, units, rows), jnp.bfloat16),
            jax.ShapeDtypeStruct((local_blocks, units, out_units), jnp.bfloat16),
        ],
    )(
        received,
        second_factor_blocks.transpose(0, 2, 1),
        second_factor_tangent.transpose(0, 2, 1),
        second_factor_blocks,
        second_factor_tangent,
    )


def curvature(
    tok_rows,
    goal_rows,
    weight,
    first_blocks,
    second_factor_blocks,
    down_blocks,
    first_tangent,
    second_factor_tangent,
):
    features = lax.axis_size("feat")
    row_count = tok_rows.shape[0]
    local_blocks, block_in, block_out = first_blocks.shape
    pair_size = block_out // (local_blocks * features)
    token_blocks = tok_rows.reshape(row_count, local_blocks, block_in)
    goal_blocks = goal_rows.reshape(row_count, local_blocks, block_in)
    split_shape = (local_blocks, block_in, features, local_blocks, pair_size)
    down_shape = (local_blocks, features, local_blocks, pair_size, block_in)
    first_act = jnp.einsum(
        "rki,kiGgc->Ggkcr",
        token_blocks,
        first_blocks.reshape(split_shape),
        preferred_element_type=jnp.float32,
    ).astype(jnp.bfloat16)
    tangents = jnp.einsum(
        "rki,kiGgc->Ggkcr",
        token_blocks,
        first_tangent.reshape(split_shape),
        preferred_element_type=jnp.float32,
    ).astype(jnp.bfloat16)
    out_grad = (
        jnp.einsum(
            "rkd,kGgcd->Ggkcr",
            goal_blocks,
            down_blocks.reshape(down_shape),
            preferred_element_type=jnp.float32,
        )
        * weight
    ).astype(jnp.bfloat16)
    merged = (features, local_blocks, local_blocks * pair_size, row_count)
    stacked = jnp.stack(
        [first_act.reshape(merged), tangents.reshape(merged), out_grad.reshape(merged)], axis=1
    )
    mixed = lax.all_to_all(stacked, "feat", split_axis=0, concat_axis=0, tiled=True)
    back_mixed, hess_mixed = second_factor(mixed, second_factor_blocks, second_factor_tangent)
    back_merged = (
        back_mixed.reshape(local_blocks, features, local_blocks, pair_size, row_count)
        .transpose(1, 2, 0, 3, 4)
        .reshape(features, local_blocks, local_blocks * pair_size, row_count)
    )
    back_first = lax.all_to_all(back_merged, "feat", split_axis=0, concat_axis=2, tiled=True)
    back_first = back_first.reshape(local_blocks, block_out, row_count)
    hess_first = jnp.einsum(
        "rki,kjr->kij", token_blocks, back_first, preferred_element_type=jnp.float32
    )
    return (hess_first, hess_mixed)


def per_device(
    tokens,
    targets,
    first_blocks,
    second_factor_blocks,
    down_blocks,
    first_tangent,
    second_factor_tangent,
    doc_lengths,
    doc_owners,
    pack_offsets,
):
    loaders = lax.axis_size("dp")
    device = lax.axis_index("dp")
    tok_count = tokens.shape[0]
    feature_cols = tokens.shape[1]
    slot_rows = 2 * tok_count // loaders
    position = jnp.arange(slot_rows, dtype=jnp.int32)
    mine = (doc_owners == device).astype(jnp.int32)
    first_row = jnp.sum(mine * pack_offsets, axis=1)
    doc_span = jnp.sum(mine * doc_lengths, axis=1)
    in_slot = position[None, :] < doc_span[:, None]
    source = jnp.where(in_slot, first_row[:, None] + position[None, :], 0)
    outgoing = jnp.take(targets, source.reshape(-1), axis=0).reshape(
        loaders, slot_rows, feature_cols
    )
    arrived = lax.all_to_all(outgoing, "dp", split_axis=0, concat_axis=0, tiled=True)
    my_lengths = lax.dynamic_index_in_dim(doc_lengths, device, 0, keepdims=False)
    my_owners = lax.dynamic_index_in_dim(doc_owners, device, 0, keepdims=False)
    my_starts = jnp.cumsum(my_lengths) - my_lengths
    token_pos = jnp.arange(tok_count, dtype=jnp.int32)
    inside = (token_pos[:, None] >= my_starts[None, :]) & (
        token_pos[:, None] < (my_starts + my_lengths)[None, :]
    )
    inside_int = inside.astype(jnp.int32)
    goal_index = (
        jnp.sum(inside_int * (my_owners * slot_rows - my_starts)[None, :], axis=1) + token_pos
    )
    weight = jnp.sum(
        inside.astype(jnp.float32) / my_lengths.astype(jnp.float32)[None, :], axis=1
    )
    goal_rows = jnp.take(
        arrived.reshape(loaders * slot_rows, feature_cols), goal_index, axis=0
    )
    hess_first, hess_mixed = curvature(
        tokens,
        goal_rows,
        weight,
        first_blocks,
        second_factor_blocks,
        down_blocks,
        first_tangent,
        second_factor_tangent,
    )
    local_blocks = hess_first.shape[0]
    first_part = hess_first.reshape(local_blocks, loaders, -1).transpose(1, 0, 2)
    mixed_part = hess_mixed.reshape(local_blocks, loaders, -1).transpose(1, 0, 2)
    first_width = first_part.shape[2]
    partials = jnp.concatenate([first_part, mixed_part], axis=2).astype(jnp.bfloat16)
    gathered = lax.all_to_all(partials, "dp", split_axis=0, concat_axis=0, tiled=True)
    total = jnp.sum(gathered.astype(jnp.float32), axis=0)
    hess_first = total[:, :first_width].reshape(local_blocks, -1, first_blocks.shape[2])
    hess_mixed = total[:, first_width:].reshape(local_blocks, -1, second_factor_blocks.shape[2])
    return (hess_first, hess_mixed)


def solution(mesh):
    in_specs = (
        P("dp", "feat"),
        P("dp", "feat"),
        P("feat", None, None),
        P("feat", None, None),
        P("feat", None, None),
        P("feat", None, None),
        P("feat", None, None),
        P(),
        P(),
        P(),
    )
    out_specs = (P("feat", "dp", None), P("feat", "dp", None))
    return jax.shard_map(
        per_device, mesh=mesh, in_specs=in_specs, out_specs=out_specs, check_vma=False
    )
```

```python
import jax
import jax.numpy as jnp
from jax import lax
from jax.sharding import PartitionSpec as P

inv_root_two = 0.7071067811865476
inv_root_two_pi = 0.3989422804014327


def curvature(
    tok_rows,
    goal_rows,
    weight,
    first_blocks,
    second_factor_blocks,
    down_blocks,
    first_tangent,
    second_factor_tangent,
):
    features = lax.axis_size("feat")
    row_count = tok_rows.shape[0]
    local_blocks, block_in, block_out = first_blocks.shape
    pair_size = block_out // (local_blocks * features)
    token_blocks = tok_rows.reshape(row_count, local_blocks, block_in)
    goal_blocks = goal_rows.reshape(row_count, local_blocks, block_in)
    split_shape = (local_blocks, block_in, features, local_blocks, pair_size)
    down_shape = (local_blocks, features, local_blocks, pair_size, block_in)
    first_act = jnp.einsum(
        "rki,kiGgc->Ggkcr",
        token_blocks,
        first_blocks.reshape(split_shape),
        preferred_element_type=jnp.float32,
    ).astype(jnp.bfloat16)
    tangents = jnp.einsum(
        "rki,kiGgc->Ggkcr",
        token_blocks,
        first_tangent.reshape(split_shape),
        preferred_element_type=jnp.float32,
    ).astype(jnp.bfloat16)
    out_grad = (
        jnp.einsum(
            "rkd,kGgcd->Ggkcr",
            goal_blocks,
            down_blocks.reshape(down_shape),
            preferred_element_type=jnp.float32,
        )
        * weight
    ).astype(jnp.bfloat16)
    merged = (features, local_blocks, local_blocks * pair_size, row_count)
    stacked = jnp.stack(
        [first_act.reshape(merged), tangents.reshape(merged), out_grad.reshape(merged)], axis=1
    )
    mixed = lax.all_to_all(stacked, "feat", split_axis=0, concat_axis=3, tiled=True)
    hidden_shape = (local_blocks, block_out, row_count)
    mixed_activation = mixed[0, 0].reshape(hidden_shape)
    mixed_tangent_value = mixed[0, 1].reshape(hidden_shape)
    hidden_grad = mixed[0, 2].reshape(hidden_shape)
    pre_act = jnp.einsum(
        "vca,vcf->vfa", mixed_activation, second_factor_blocks, preferred_element_type=jnp.float32
    )
    pre_tan = jnp.einsum(
        "vca,vcf->vfa",
        mixed_tangent_value,
        second_factor_blocks,
        preferred_element_type=jnp.float32,
    ) + jnp.einsum(
        "vca,vcf->vfa", mixed_activation, second_factor_tangent, preferred_element_type=jnp.float32
    )
    density = jnp.exp(-0.5 * pre_act * pre_act) * inv_root_two_pi
    normal_cdf = 0.5 * (1.0 + lax.erf(pre_act * inv_root_two))
    preactivation_gradient = (hidden_grad * (normal_cdf + pre_act * density)).astype(jnp.bfloat16)
    preactivation_tangent_gradient = (
        hidden_grad * (density * (2.0 - pre_act * pre_act)) * pre_tan
    ).astype(jnp.bfloat16)
    hess_mixed = jnp.einsum(
        "evp,eqp->evq",
        mixed_tangent_value,
        preactivation_gradient,
        preferred_element_type=jnp.float32,
    ) + jnp.einsum(
        "evp,eqp->evq",
        mixed_activation,
        preactivation_tangent_gradient,
        preferred_element_type=jnp.float32,
    )
    pos_shape = (local_blocks, features, local_blocks, pair_size, block_out)
    back_mixed = jnp.einsum(
        "bip,bFkci->Fkbcp",
        preactivation_tangent_gradient,
        second_factor_blocks.reshape(pos_shape),
        preferred_element_type=jnp.float32,
    ) + jnp.einsum(
        "bip,bFkci->Fkbcp",
        preactivation_gradient,
        second_factor_tangent.reshape(pos_shape),
        preferred_element_type=jnp.float32,
    )
    back_merged = back_mixed.astype(jnp.bfloat16).reshape(
        features, local_blocks, local_blocks * pair_size, row_count
    )
    back_first = lax.all_to_all(back_merged, "feat", split_axis=0, concat_axis=2, tiled=True)
    back_first = back_first.reshape(local_blocks, block_out, row_count)
    hess_first = jnp.einsum(
        "rki,kjr->kij", token_blocks, back_first, preferred_element_type=jnp.float32
    )
    return (hess_first, hess_mixed)


def per_device(
    tokens,
    targets,
    first_blocks,
    second_factor_blocks,
    down_blocks,
    first_tangent,
    second_factor_tangent,
    doc_lengths,
    doc_owners,
    pack_offsets,
):
    loaders = lax.axis_size("dp")
    device = lax.axis_index("dp")
    tok_count = tokens.shape[0]
    feature_cols = tokens.shape[1]
    slot_rows = 2 * tok_count // loaders
    position = jnp.arange(slot_rows, dtype=jnp.int32)
    mine = (doc_owners == device).astype(jnp.int32)
    first_row = jnp.sum(mine * pack_offsets, axis=1)
    doc_span = jnp.sum(mine * doc_lengths, axis=1)
    in_slot = position[None, :] < doc_span[:, None]
    source = jnp.where(in_slot, first_row[:, None] + position[None, :], 0)
    outgoing = targets.at[source.reshape(-1)].get(mode="promise_in_bounds").reshape(
        loaders, slot_rows, feature_cols
    )
    arrived = lax.all_to_all(outgoing, "dp", split_axis=0, concat_axis=0, tiled=True)
    my_lengths = lax.dynamic_index_in_dim(doc_lengths, device, 0, keepdims=False)
    my_owners = lax.dynamic_index_in_dim(doc_owners, device, 0, keepdims=False)
    my_starts = jnp.cumsum(my_lengths) - my_lengths
    token_pos = jnp.arange(tok_count, dtype=jnp.int32)
    inside = (token_pos[:, None] >= my_starts[None, :]) & (
        token_pos[:, None] < (my_starts + my_lengths)[None, :]
    )
    inside_int = inside.astype(jnp.int32)
    goal_index = (
        jnp.sum(inside_int * (my_owners * slot_rows - my_starts)[None, :], axis=1) + token_pos
    )
    weight = jnp.sum(
        inside.astype(jnp.float32) / my_lengths.astype(jnp.float32)[None, :], axis=1
    )
    goal_rows = (
        arrived.reshape(loaders * slot_rows, feature_cols)
        .at[goal_index]
        .get(mode="promise_in_bounds")
    )
    hess_first, hess_mixed = curvature(
        tokens,
        goal_rows,
        weight,
        first_blocks,
        second_factor_blocks,
        down_blocks,
        first_tangent,
        second_factor_tangent,
    )
    local_blocks = hess_first.shape[0]
    first_part = hess_first.reshape(local_blocks, loaders, -1).transpose(1, 0, 2)
    mixed_part = hess_mixed.reshape(local_blocks, loaders, -1).transpose(1, 0, 2)
    first_width = first_part.shape[2]
    partials = jnp.concatenate([first_part, mixed_part], axis=2).astype(jnp.bfloat16)
    gathered = lax.all_to_all(partials, "dp", split_axis=0, concat_axis=0, tiled=True)
    total = jnp.sum(gathered.astype(jnp.float32), axis=0)
    hess_first = total[:, :first_width].reshape(local_blocks, -1, first_blocks.shape[2])
    hess_mixed = total[:, first_width:].reshape(local_blocks, -1, second_factor_blocks.shape[2])
    return (hess_first, hess_mixed)


def solution(mesh):
    in_specs = (
        P("dp", "feat"),
        P("dp", "feat"),
        P("feat", None, None),
        P("feat", None, None),
        P("feat", None, None),
        P("feat", None, None),
        P("feat", None, None),
        P(),
        P(),
        P(),
    )
    out_specs = (P("feat", "dp", None), P("feat", "dp", None))
    return jax.shard_map(
        per_device, mesh=mesh, in_specs=in_specs, out_specs=out_specs, check_vma=False
    )
```

```python
import jax
import jax.numpy as jnp
from jax import lax
from jax.sharding import Mesh, PartitionSpec as P

DP = ("y", "x")
FE = ("z", "core")

inv_root_two = 0.7071067811865476
inv_root_two_pi = 0.3989422804014327


def curvature(
    tok_rows,
    goal_rows,
    weight,
    first_blocks,
    second_factor_blocks,
    down_blocks,
    first_tangent,
    second_factor_tangent,
):
    features = lax.axis_size(FE)
    row_count = tok_rows.shape[0]
    local_blocks, block_in, block_out = first_blocks.shape
    pair_size = block_out // (local_blocks * features)
    token_blocks = tok_rows.reshape(row_count, local_blocks, block_in)
    goal_blocks = goal_rows.reshape(row_count, local_blocks, block_in)
    split_shape = (local_blocks, block_in, features, local_blocks, pair_size)
    down_shape = (local_blocks, features, local_blocks, pair_size, block_in)
    first_act = jnp.einsum(
        "rki,kiGgc->Ggkcr",
        token_blocks,
        first_blocks.reshape(split_shape),
        preferred_element_type=jnp.float32,
    ).astype(jnp.bfloat16)
    tangents = jnp.einsum(
        "rki,kiGgc->Ggkcr",
        token_blocks,
        first_tangent.reshape(split_shape),
        preferred_element_type=jnp.float32,
    ).astype(jnp.bfloat16)
    out_grad = (
        jnp.einsum(
            "rkd,kGgcd->Ggkcr",
            goal_blocks,
            down_blocks.reshape(down_shape),
            preferred_element_type=jnp.float32,
        )
        * weight
    ).astype(jnp.bfloat16)
    merged = (features, local_blocks, local_blocks * pair_size, row_count)
    stacked = jnp.stack(
        [first_act.reshape(merged), tangents.reshape(merged), out_grad.reshape(merged)], axis=1
    )
    mixed = lax.all_to_all(stacked, FE, split_axis=0, concat_axis=3, tiled=True)
    hidden_shape = (local_blocks, block_out, row_count)
    mixed_activation = mixed[0, 0].reshape(hidden_shape)
    mixed_tangent_value = mixed[0, 1].reshape(hidden_shape)
    hidden_grad = mixed[0, 2].reshape(hidden_shape)
    pre_act = jnp.einsum(
        "vca,vcf->vfa", mixed_activation, second_factor_blocks, preferred_element_type=jnp.float32
    )
    pre_tan = jnp.einsum(
        "vca,vcf->vfa",
        mixed_tangent_value,
        second_factor_blocks,
        preferred_element_type=jnp.float32,
    ) + jnp.einsum(
        "vca,vcf->vfa", mixed_activation, second_factor_tangent, preferred_element_type=jnp.float32
    )
    density = jnp.exp(-0.5 * pre_act * pre_act) * inv_root_two_pi
    normal_cdf = 0.5 * (1.0 + lax.erf(pre_act * inv_root_two))
    preactivation_gradient = (hidden_grad * (normal_cdf + pre_act * density)).astype(jnp.bfloat16)
    preactivation_tangent_gradient = (
        hidden_grad * (density * (2.0 - pre_act * pre_act)) * pre_tan
    ).astype(jnp.bfloat16)
    hess_mixed = jnp.einsum(
        "evp,eqp->evq",
        mixed_tangent_value,
        preactivation_gradient,
        preferred_element_type=jnp.float32,
    ) + jnp.einsum(
        "evp,eqp->evq",
        mixed_activation,
        preactivation_tangent_gradient,
        preferred_element_type=jnp.float32,
    )
    pos_shape = (local_blocks, features, local_blocks, pair_size, block_out)
    back_mixed = jnp.einsum(
        "bip,bFkci->Fkbcp",
        preactivation_tangent_gradient,
        second_factor_blocks.reshape(pos_shape),
        preferred_element_type=jnp.float32,
    ) + jnp.einsum(
        "bip,bFkci->Fkbcp",
        preactivation_gradient,
        second_factor_tangent.reshape(pos_shape),
        preferred_element_type=jnp.float32,
    )
    back_merged = back_mixed.astype(jnp.bfloat16).reshape(
        features, local_blocks, local_blocks * pair_size, row_count
    )
    back_first = lax.all_to_all(back_merged, FE, split_axis=0, concat_axis=2, tiled=True)
    back_first = back_first.reshape(local_blocks, block_out, row_count)
    hess_first = jnp.einsum(
        "rki,kjr->kij", token_blocks, back_first, preferred_element_type=jnp.float32
    )
    return (hess_first, hess_mixed)


def per_device(
    tokens,
    targets,
    first_blocks,
    second_factor_blocks,
    down_blocks,
    first_tangent,
    second_factor_tangent,
    doc_lengths,
    doc_owners,
    pack_offsets,
):
    loaders = lax.axis_size(DP)
    device = lax.axis_index(DP)
    tok_count = tokens.shape[0]
    feature_cols = tokens.shape[1]
    slot_rows = 2 * tok_count // loaders
    position = jnp.arange(slot_rows, dtype=jnp.int32)
    mine = (doc_owners == device).astype(jnp.int32)
    first_row = jnp.sum(mine * pack_offsets, axis=1)
    doc_span = jnp.sum(mine * doc_lengths, axis=1)
    in_slot = position[None, :] < doc_span[:, None]
    source = jnp.where(in_slot, first_row[:, None] + position[None, :], 0)
    outgoing = jnp.take(targets, source.reshape(-1), axis=0).reshape(
        loaders, slot_rows, feature_cols
    )
    arrived = lax.all_to_all(outgoing, DP, split_axis=0, concat_axis=0, tiled=True)
    my_lengths = lax.dynamic_index_in_dim(doc_lengths, device, 0, keepdims=False)
    my_owners = lax.dynamic_index_in_dim(doc_owners, device, 0, keepdims=False)
    my_starts = jnp.cumsum(my_lengths) - my_lengths
    token_pos = jnp.arange(tok_count, dtype=jnp.int32)
    inside = (token_pos[:, None] >= my_starts[None, :]) & (
        token_pos[:, None] < (my_starts + my_lengths)[None, :]
    )
    inside_int = inside.astype(jnp.int32)
    goal_index = (
        jnp.sum(inside_int * (my_owners * slot_rows - my_starts)[None, :], axis=1) + token_pos
    )
    weight = jnp.sum(
        inside.astype(jnp.float32) / my_lengths.astype(jnp.float32)[None, :], axis=1
    )
    goal_rows = jnp.take(
        arrived.reshape(loaders * slot_rows, feature_cols), goal_index, axis=0
    )
    hess_first, hess_mixed = curvature(
        tokens,
        goal_rows,
        weight,
        first_blocks,
        second_factor_blocks,
        down_blocks,
        first_tangent,
        second_factor_tangent,
    )
    local_blocks = hess_first.shape[0]
    first_part = hess_first.reshape(local_blocks, loaders, -1).transpose(1, 0, 2)
    mixed_part = hess_mixed.reshape(local_blocks, loaders, -1).transpose(1, 0, 2)
    first_width = first_part.shape[2]
    partials = jnp.concatenate([first_part, mixed_part], axis=2).astype(jnp.bfloat16)
    x_size = lax.axis_size("x")
    partials = partials.reshape(loaders // x_size, x_size, *partials.shape[1:])
    across_x = lax.all_to_all(partials, "x", split_axis=1, concat_axis=1, tiled=True)
    row_sums = jnp.sum(across_x.astype(jnp.float32), axis=1).astype(jnp.bfloat16)
    across_y = lax.all_to_all(row_sums, "y", split_axis=0, concat_axis=0, tiled=True)
    total = jnp.sum(across_y.astype(jnp.float32), axis=0)
    hess_first = total[:, :first_width].reshape(local_blocks, -1, first_blocks.shape[2])
    hess_mixed = total[:, first_width:].reshape(local_blocks, -1, second_factor_blocks.shape[2])
    return (hess_first, hess_mixed)


def solution(mesh):
    dp_size, feat_size = mesh.shape["dp"], mesh.shape["feat"]
    x_size = 4
    view = Mesh(
        mesh.devices.reshape(dp_size // x_size, x_size, feat_size // 2, 2),
        ("y", "x", "z", "core"),
    )
    in_specs = (
        P(DP, FE),
        P(DP, FE),
        P(FE, None, None),
        P(FE, None, None),
        P(FE, None, None),
        P(FE, None, None),
        P(FE, None, None),
        P(),
        P(),
        P(),
    )
    out_specs = (P(FE, DP, None), P(FE, DP, None))
    return jax.shard_map(
        per_device, mesh=view, in_specs=in_specs, out_specs=out_specs, check_vma=False
    )
```

```python
import jax
import jax.numpy as jnp
from jax import lax
from jax.sharding import Mesh, PartitionSpec as P

DP = ("y", "x")
FE = ("z", "core")

inv_root_two = 0.7071067811865476
inv_root_two_pi = 0.3989422804014327


def curvature(
    tok_rows,
    goal_rows,
    weight,
    first_blocks,
    second_factor_blocks,
    down_blocks,
    first_tangent,
    second_factor_tangent,
):
    features = lax.axis_size(FE)
    row_count = tok_rows.shape[0]
    local_blocks, block_in, block_out = first_blocks.shape
    pair_size = block_out // (local_blocks * features)
    token_blocks = tok_rows.reshape(row_count, local_blocks, block_in)
    goal_blocks = goal_rows.reshape(local_blocks, block_in, row_count)
    split_shape = (local_blocks, block_in, features, local_blocks, pair_size)
    down_shape = (local_blocks, features, local_blocks, pair_size, block_in)
    first_act = jnp.einsum(
        "rki,kiGgc->Ggkcr",
        token_blocks,
        first_blocks.reshape(split_shape),
        preferred_element_type=jnp.float32,
    ).astype(jnp.bfloat16)
    tangents = jnp.einsum(
        "rki,kiGgc->Ggkcr",
        token_blocks,
        first_tangent.reshape(split_shape),
        preferred_element_type=jnp.float32,
    ).astype(jnp.bfloat16)
    out_grad = (
        jnp.einsum(
            "kdr,kGgcd->Ggkcr",
            goal_blocks,
            down_blocks.reshape(down_shape),
            preferred_element_type=jnp.float32,
        )
        * weight
    ).astype(jnp.bfloat16)
    merged = (features, local_blocks, local_blocks * pair_size, row_count)
    stacked = jnp.stack(
        [first_act.reshape(merged), tangents.reshape(merged), out_grad.reshape(merged)], axis=1
    )
    mixed = lax.all_to_all(stacked, FE, split_axis=0, concat_axis=3, tiled=True)
    hidden_shape = (local_blocks, block_out, row_count)
    mixed_activation = mixed[0, 0].reshape(hidden_shape)
    mixed_tangent_value = mixed[0, 1].reshape(hidden_shape)
    hidden_grad = mixed[0, 2].reshape(hidden_shape)
    pre_act = jnp.einsum(
        "vca,vcf->vfa", mixed_activation, second_factor_blocks, preferred_element_type=jnp.float32
    )
    pre_tan = jnp.einsum(
        "vca,vcf->vfa",
        mixed_tangent_value,
        second_factor_blocks,
        preferred_element_type=jnp.float32,
    ) + jnp.einsum(
        "vca,vcf->vfa", mixed_activation, second_factor_tangent, preferred_element_type=jnp.float32
    )
    density = jnp.exp(-0.5 * pre_act * pre_act) * inv_root_two_pi
    normal_cdf = 0.5 * (1.0 + lax.erf(pre_act * inv_root_two))
    preactivation_gradient = (hidden_grad * (normal_cdf + pre_act * density)).astype(jnp.bfloat16)
    preactivation_tangent_gradient = (
        hidden_grad * (density * (2.0 - pre_act * pre_act)) * pre_tan
    ).astype(jnp.bfloat16)
    hess_mixed = jnp.einsum(
        "evp,eqp->evq",
        mixed_tangent_value,
        preactivation_gradient,
        preferred_element_type=jnp.float32,
    ) + jnp.einsum(
        "evp,eqp->evq",
        mixed_activation,
        preactivation_tangent_gradient,
        preferred_element_type=jnp.float32,
    )
    pos_shape = (local_blocks, features, local_blocks, pair_size, block_out)
    back_mixed = jnp.einsum(
        "bip,bFkci->Fkbcp",
        preactivation_tangent_gradient,
        second_factor_blocks.reshape(pos_shape),
        preferred_element_type=jnp.float32,
    ) + jnp.einsum(
        "bip,bFkci->Fkbcp",
        preactivation_gradient,
        second_factor_tangent.reshape(pos_shape),
        preferred_element_type=jnp.float32,
    )
    back_merged = back_mixed.astype(jnp.bfloat16).reshape(
        features, local_blocks, local_blocks * pair_size, row_count
    )
    back_first = lax.all_to_all(back_merged, FE, split_axis=0, concat_axis=2, tiled=True)
    back_first = back_first.reshape(local_blocks, block_out, row_count)
    hess_first = jnp.einsum(
        "rki,kjr->kij", token_blocks, back_first, preferred_element_type=jnp.float32
    )
    return (hess_first, hess_mixed)


def per_device(
    tokens,
    targets,
    first_blocks,
    second_factor_blocks,
    down_blocks,
    first_tangent,
    second_factor_tangent,
    doc_lengths,
    doc_owners,
    pack_offsets,
):
    loaders = lax.axis_size(DP)
    device = lax.axis_index(DP)
    tok_count = tokens.shape[0]
    feature_cols = tokens.shape[1]
    slot_rows = 2 * tok_count // loaders
    position = jnp.arange(slot_rows, dtype=jnp.int32)
    mine = (doc_owners == device).astype(jnp.int32)
    first_row = jnp.sum(mine * pack_offsets, axis=1)
    doc_span = jnp.sum(mine * doc_lengths, axis=1)
    in_slot = position[None, :] < doc_span[:, None]
    source = jnp.where(in_slot, first_row[:, None] + position[None, :], 0)
    outgoing = jnp.take(targets, source.reshape(-1), axis=0).reshape(
        loaders, slot_rows, feature_cols
    )
    arrived = lax.all_to_all(outgoing, DP, split_axis=0, concat_axis=0, tiled=True)
    my_lengths = lax.dynamic_index_in_dim(doc_lengths, device, 0, keepdims=False)
    my_owners = lax.dynamic_index_in_dim(doc_owners, device, 0, keepdims=False)
    my_starts = jnp.cumsum(my_lengths) - my_lengths
    token_pos = jnp.arange(tok_count, dtype=jnp.int32)
    inside = (token_pos[:, None] >= my_starts[None, :]) & (
        token_pos[:, None] < (my_starts + my_lengths)[None, :]
    )
    inside_int = inside.astype(jnp.int32)
    goal_index = (
        jnp.sum(inside_int * (my_owners * slot_rows - my_starts)[None, :], axis=1) + token_pos
    )
    weight = jnp.sum(
        inside.astype(jnp.float32) / my_lengths.astype(jnp.float32)[None, :], axis=1
    )
    picks = (
        jnp.arange(loaders * slot_rows, dtype=jnp.int32)[:, None] == goal_index[None, :]
    ).astype(jnp.bfloat16)
    goal_cols = lax.dot_general(
        arrived.reshape(loaders * slot_rows, feature_cols),
        picks,
        (((0,), (0,)), ((), ())),
        preferred_element_type=jnp.float32,
    ).astype(jnp.bfloat16)
    hess_first, hess_mixed = curvature(
        tokens,
        goal_cols,
        weight,
        first_blocks,
        second_factor_blocks,
        down_blocks,
        first_tangent,
        second_factor_tangent,
    )
    local_blocks = hess_first.shape[0]
    first_part = hess_first.reshape(local_blocks, loaders, -1).transpose(1, 0, 2)
    mixed_part = hess_mixed.reshape(local_blocks, loaders, -1).transpose(1, 0, 2)
    first_width = first_part.shape[2]
    partials = jnp.concatenate([first_part, mixed_part], axis=2).astype(jnp.bfloat16)
    x_size = lax.axis_size("x")
    partials = partials.reshape(loaders // x_size, x_size, *partials.shape[1:])
    across_x = lax.all_to_all(partials, "x", split_axis=1, concat_axis=1, tiled=True)
    row_sums = jnp.sum(across_x.astype(jnp.float32), axis=1).astype(jnp.bfloat16)
    across_y = lax.all_to_all(row_sums, "y", split_axis=0, concat_axis=0, tiled=True)
    total = jnp.sum(across_y.astype(jnp.float32), axis=0)
    hess_first = total[:, :first_width].reshape(local_blocks, -1, first_blocks.shape[2])
    hess_mixed = total[:, first_width:].reshape(local_blocks, -1, second_factor_blocks.shape[2])
    return (hess_first, hess_mixed)


def solution(mesh):
    dp_size, feat_size = mesh.shape["dp"], mesh.shape["feat"]
    x_size = 4
    view = Mesh(
        mesh.devices.reshape(dp_size // x_size, x_size, feat_size // 2, 2),
        ("y", "x", "z", "core"),
    )
    in_specs = (
        P(DP, FE),
        P(DP, FE),
        P(FE, None, None),
        P(FE, None, None),
        P(FE, None, None),
        P(FE, None, None),
        P(FE, None, None),
        P(),
        P(),
        P(),
    )
    out_specs = (P(FE, DP, None), P(FE, DP, None))
    return jax.shard_map(
        per_device, mesh=view, in_specs=in_specs, out_specs=out_specs, check_vma=False
    )
```

```python
import jax
import jax.numpy as jnp
from jax import lax
from jax.sharding import Mesh, PartitionSpec as P

DP = ("y", "x")
FE = ("z", "core")

inv_root_two = 0.7071067811865476
inv_root_two_pi = 0.3989422804014327


def curvature(
    tok_rows,
    goal_rows,
    weight,
    first_blocks,
    second_factor_blocks,
    down_blocks,
    first_tangent,
    second_factor_tangent,
):
    features = lax.axis_size(FE)
    row_count = tok_rows.shape[0]
    local_blocks, block_in, block_out = first_blocks.shape
    pair_size = block_out // (local_blocks * features)
    token_blocks = tok_rows.reshape(row_count, local_blocks, block_in)
    goal_blocks = goal_rows.reshape(local_blocks, block_in, row_count)
    split_shape = (local_blocks, block_in, features, local_blocks, pair_size)
    down_shape = (local_blocks, features, local_blocks, pair_size, block_in)
    first_act = jnp.einsum(
        "rki,kiGgc->Ggkcr",
        token_blocks,
        first_blocks.reshape(split_shape),
        preferred_element_type=jnp.float32,
    ).astype(jnp.bfloat16)
    tangents = jnp.einsum(
        "rki,kiGgc->Ggkcr",
        token_blocks,
        first_tangent.reshape(split_shape),
        preferred_element_type=jnp.float32,
    ).astype(jnp.bfloat16)
    out_grad = (
        jnp.einsum(
            "kdr,kGgcd->Ggkcr",
            goal_blocks,
            down_blocks.reshape(down_shape),
            preferred_element_type=jnp.float32,
        )
        * weight
    ).astype(jnp.bfloat16)
    merged = (features, local_blocks, local_blocks * pair_size, row_count)
    stacked = jnp.stack(
        [first_act.reshape(merged), tangents.reshape(merged), out_grad.reshape(merged)], axis=1
    )
    mixed = lax.all_to_all(stacked, FE, split_axis=0, concat_axis=3, tiled=True)
    hidden_shape = (local_blocks, block_out, row_count)
    mixed_activation = mixed[0, 0].reshape(hidden_shape)
    mixed_tangent_value = mixed[0, 1].reshape(hidden_shape)
    hidden_grad = mixed[0, 2].reshape(hidden_shape)
    pre_act = jnp.einsum(
        "vca,vcf->vfa", mixed_activation, second_factor_blocks, preferred_element_type=jnp.float32
    )
    pre_tan = jnp.einsum(
        "vca,vcf->vfa",
        mixed_tangent_value,
        second_factor_blocks,
        preferred_element_type=jnp.float32,
    ) + jnp.einsum(
        "vca,vcf->vfa", mixed_activation, second_factor_tangent, preferred_element_type=jnp.float32
    )
    density = jnp.exp(-0.5 * pre_act * pre_act) * inv_root_two_pi
    normal_cdf = 0.5 * (1.0 + lax.erf(pre_act * inv_root_two))
    preactivation_gradient = (hidden_grad * (normal_cdf + pre_act * density)).astype(jnp.bfloat16)
    preactivation_tangent_gradient = (
        hidden_grad * (density * (2.0 - pre_act * pre_act)) * pre_tan
    ).astype(jnp.bfloat16)
    hess_mixed = jnp.einsum(
        "evp,eqp->evq",
        mixed_tangent_value,
        preactivation_gradient,
        preferred_element_type=jnp.float32,
    ) + jnp.einsum(
        "evp,eqp->evq",
        mixed_activation,
        preactivation_tangent_gradient,
        preferred_element_type=jnp.float32,
    )
    pos_shape = (local_blocks, features, local_blocks, pair_size, block_out)
    back_mixed = jnp.einsum(
        "bip,bFkci->Fkbcp",
        preactivation_tangent_gradient,
        second_factor_blocks.reshape(pos_shape),
        preferred_element_type=jnp.float32,
    ) + jnp.einsum(
        "bip,bFkci->Fkbcp",
        preactivation_gradient,
        second_factor_tangent.reshape(pos_shape),
        preferred_element_type=jnp.float32,
    )
    back_merged = back_mixed.astype(jnp.bfloat16).reshape(
        features, local_blocks, local_blocks * pair_size, row_count
    )
    loaders = lax.axis_size(DP)
    x_size = lax.axis_size("x")
    me_x = lax.axis_index("x")
    mixed_part = (
        hess_mixed.reshape(local_blocks, loaders, -1)
        .transpose(1, 0, 2)
        .astype(jnp.bfloat16)
        .reshape(loaders // x_size, x_size, local_blocks, -1)
    )
    mixed_rows = lax.dynamic_index_in_dim(mixed_part, me_x, 1, keepdims=False).astype(
        jnp.float32
    )
    for shift in range(1, x_size):
        piece = lax.dynamic_index_in_dim(mixed_part, (me_x + shift) % x_size, 1, keepdims=False)
        moved = lax.ppermute(piece, "x", [(i, (i + shift) % x_size) for i in range(x_size)])
        mixed_rows = mixed_rows + moved.astype(jnp.float32)
    back_first = lax.all_to_all(back_merged, FE, split_axis=0, concat_axis=2, tiled=True)
    back_first = back_first.reshape(local_blocks, block_out, row_count)
    hess_first = jnp.einsum(
        "rki,kjr->kij", token_blocks, back_first, preferred_element_type=jnp.float32
    )
    return (hess_first, mixed_rows)


def per_device(
    tokens,
    targets,
    first_blocks,
    second_factor_blocks,
    down_blocks,
    first_tangent,
    second_factor_tangent,
    doc_lengths,
    doc_owners,
    pack_offsets,
):
    loaders = lax.axis_size(DP)
    device = lax.axis_index(DP)
    tok_count = tokens.shape[0]
    feature_cols = tokens.shape[1]
    slot_rows = 2 * tok_count // loaders
    position = jnp.arange(slot_rows, dtype=jnp.int32)
    mine = (doc_owners == device).astype(jnp.int32)
    first_row = jnp.sum(mine * pack_offsets, axis=1)
    doc_span = jnp.sum(mine * doc_lengths, axis=1)
    in_slot = position[None, :] < doc_span[:, None]
    source = jnp.where(in_slot, first_row[:, None] + position[None, :], 0)
    outgoing = jnp.take(targets, source.reshape(-1), axis=0).reshape(
        loaders, slot_rows, feature_cols
    )
    arrived = lax.all_to_all(outgoing, DP, split_axis=0, concat_axis=0, tiled=True)
    my_lengths = lax.dynamic_index_in_dim(doc_lengths, device, 0, keepdims=False)
    my_owners = lax.dynamic_index_in_dim(doc_owners, device, 0, keepdims=False)
    my_starts = jnp.cumsum(my_lengths) - my_lengths
    token_pos = jnp.arange(tok_count, dtype=jnp.int32)
    inside = (token_pos[:, None] >= my_starts[None, :]) & (
        token_pos[:, None] < (my_starts + my_lengths)[None, :]
    )
    inside_int = inside.astype(jnp.int32)
    goal_index = (
        jnp.sum(inside_int * (my_owners * slot_rows - my_starts)[None, :], axis=1) + token_pos
    )
    weight = jnp.sum(
        inside.astype(jnp.float32) / my_lengths.astype(jnp.float32)[None, :], axis=1
    )
    picks = (
        jnp.arange(loaders * slot_rows, dtype=jnp.int32)[:, None] == goal_index[None, :]
    ).astype(jnp.bfloat16)
    goal_cols = lax.dot_general(
        arrived.reshape(loaders * slot_rows, feature_cols),
        picks,
        (((0,), (0,)), ((), ())),
        preferred_element_type=jnp.float32,
    ).astype(jnp.bfloat16)
    hess_first, mixed_rows = curvature(
        tokens,
        goal_cols,
        weight,
        first_blocks,
        second_factor_blocks,
        down_blocks,
        first_tangent,
        second_factor_tangent,
    )
    local_blocks = hess_first.shape[0]
    x_size = lax.axis_size("x")
    first_part = (
        hess_first.reshape(local_blocks, loaders, -1)
        .transpose(1, 0, 2)
        .astype(jnp.bfloat16)
        .reshape(loaders // x_size, x_size, local_blocks, -1)
    )
    first_width = first_part.shape[3]
    across_x = lax.all_to_all(first_part, "x", split_axis=1, concat_axis=1, tiled=True)
    first_rows = jnp.sum(across_x.astype(jnp.float32), axis=1)
    row_sums = jnp.concatenate([first_rows, mixed_rows], axis=2).astype(jnp.bfloat16)
    across_y = lax.all_to_all(row_sums, "y", split_axis=0, concat_axis=0, tiled=True)
    total = jnp.sum(across_y.astype(jnp.float32), axis=0)
    hess_first = total[:, :first_width].reshape(local_blocks, -1, first_blocks.shape[2])
    hess_mixed = total[:, first_width:].reshape(local_blocks, -1, second_factor_blocks.shape[2])
    return (hess_first, hess_mixed)


def solution(mesh):
    dp_size, feat_size = mesh.shape["dp"], mesh.shape["feat"]
    x_size = 4
    view = Mesh(
        mesh.devices.reshape(dp_size // x_size, x_size, feat_size // 2, 2),
        ("y", "x", "z", "core"),
    )
    in_specs = (
        P(DP, FE),
        P(DP, FE),
        P(FE, None, None),
        P(FE, None, None),
        P(FE, None, None),
        P(FE, None, None),
        P(FE, None, None),
        P(),
        P(),
        P(),
    )
    out_specs = (P(FE, DP, None), P(FE, DP, None))
    return jax.shard_map(
        per_device, mesh=view, in_specs=in_specs, out_specs=out_specs, check_vma=False
    )
```

```python
import jax
import jax.numpy as jnp
from jax import lax
from jax.sharding import Mesh, PartitionSpec as P

DP = ("y", "x")
FE = ("z", "core")

inv_root_two = 0.7071067811865476
inv_root_two_pi = 0.3989422804014327


def curvature(
    tok_rows,
    goal_rows,
    weight,
    first_blocks,
    second_factor_blocks,
    down_blocks,
    first_tangent,
    second_factor_tangent,
):
    features = lax.axis_size(FE)
    row_count = tok_rows.shape[0]
    local_blocks, block_in, block_out = first_blocks.shape
    pair_size = block_out // (local_blocks * features)
    token_blocks = tok_rows.reshape(row_count, local_blocks, block_in)
    goal_blocks = goal_rows.reshape(local_blocks, block_in, row_count)
    split_shape = (local_blocks, block_in, features, local_blocks, pair_size)
    down_shape = (local_blocks, features, local_blocks, pair_size, block_in)
    first_act = jnp.einsum(
        "rki,kiGgc->Ggkcr",
        token_blocks,
        first_blocks.reshape(split_shape),
        preferred_element_type=jnp.float32,
    ).astype(jnp.bfloat16)
    tangents = jnp.einsum(
        "rki,kiGgc->Ggkcr",
        token_blocks,
        first_tangent.reshape(split_shape),
        preferred_element_type=jnp.float32,
    ).astype(jnp.bfloat16)
    out_grad = (
        jnp.einsum(
            "kdr,kGgcd->Ggkcr",
            goal_blocks,
            down_blocks.reshape(down_shape),
            preferred_element_type=jnp.float32,
        )
        * weight
    ).astype(jnp.bfloat16)
    merged = (features, local_blocks, local_blocks * pair_size, row_count)
    stacked = jnp.stack(
        [first_act.reshape(merged), tangents.reshape(merged), out_grad.reshape(merged)], axis=1
    )
    mixed = lax.all_to_all(stacked, FE, split_axis=0, concat_axis=3, tiled=True)
    hidden_shape = (local_blocks, block_out, row_count)
    mixed_activation = mixed[0, 0].reshape(hidden_shape)
    mixed_tangent_value = mixed[0, 1].reshape(hidden_shape)
    hidden_grad = mixed[0, 2].reshape(hidden_shape)
    pre_act = jnp.einsum(
        "vca,vcf->vfa", mixed_activation, second_factor_blocks, preferred_element_type=jnp.float32
    )
    pre_tan = jnp.einsum(
        "vca,vcf->vfa",
        mixed_tangent_value,
        second_factor_blocks,
        preferred_element_type=jnp.float32,
    ) + jnp.einsum(
        "vca,vcf->vfa", mixed_activation, second_factor_tangent, preferred_element_type=jnp.float32
    )
    density = jnp.exp(-0.5 * pre_act * pre_act) * inv_root_two_pi
    normal_cdf = 0.5 * (1.0 + lax.erf(pre_act * inv_root_two))
    preactivation_gradient = (hidden_grad * (normal_cdf + pre_act * density)).astype(jnp.bfloat16)
    preactivation_tangent_gradient = (
        hidden_grad * (density * (2.0 - pre_act * pre_act)) * pre_tan
    ).astype(jnp.bfloat16)
    hess_mixed = jnp.einsum(
        "evp,eqp->evq",
        mixed_tangent_value,
        preactivation_gradient,
        preferred_element_type=jnp.float32,
    ) + jnp.einsum(
        "evp,eqp->evq",
        mixed_activation,
        preactivation_tangent_gradient,
        preferred_element_type=jnp.float32,
    )
    pos_shape = (local_blocks, features, local_blocks, pair_size, block_out)
    back_mixed = jnp.einsum(
        "bip,bFkci->Fkbcp",
        preactivation_tangent_gradient,
        second_factor_blocks.reshape(pos_shape),
        preferred_element_type=jnp.float32,
    ) + jnp.einsum(
        "bip,bFkci->Fkbcp",
        preactivation_gradient,
        second_factor_tangent.reshape(pos_shape),
        preferred_element_type=jnp.float32,
    )
    back_merged = back_mixed.astype(jnp.bfloat16).reshape(
        features, local_blocks, local_blocks * pair_size, row_count
    )
    loaders = lax.axis_size(DP)
    x_size = lax.axis_size("x")
    me_x = lax.axis_index("x")
    mixed_part = (
        hess_mixed.reshape(local_blocks, loaders, -1)
        .transpose(1, 0, 2)
        .astype(jnp.bfloat16)
        .reshape(loaders // x_size, x_size, local_blocks, -1)
    )
    mixed_rows = lax.dynamic_index_in_dim(mixed_part, me_x, 1, keepdims=False).astype(
        jnp.float32
    )
    for shift in range(1, x_size):
        piece = lax.dynamic_index_in_dim(mixed_part, (me_x + shift) % x_size, 1, keepdims=False)
        moved = lax.ppermute(piece, "x", [(i, (i + shift) % x_size) for i in range(x_size)])
        mixed_rows = mixed_rows + moved.astype(jnp.float32)
    back_first = lax.all_to_all(back_merged, FE, split_axis=0, concat_axis=2, tiled=True)
    back_first = back_first.reshape(local_blocks, block_out, row_count)
    hess_first = jnp.einsum(
        "rki,kjr->kij", token_blocks, back_first, preferred_element_type=jnp.float32
    )
    return (hess_first, mixed_rows)


def per_device(
    tokens,
    targets,
    first_blocks,
    second_factor_blocks,
    down_blocks,
    first_tangent,
    second_factor_tangent,
    doc_lengths,
    doc_owners,
    pack_offsets,
):
    loaders = lax.axis_size(DP)
    device = lax.axis_index(DP)
    tok_count = tokens.shape[0]
    feature_cols = tokens.shape[1]
    slot_rows = 2 * tok_count // loaders
    position = jnp.arange(slot_rows, dtype=jnp.int32)
    mine = (doc_owners == device).astype(jnp.int32)
    first_row = jnp.sum(mine * pack_offsets, axis=1)
    doc_span = jnp.sum(mine * doc_lengths, axis=1)
    in_slot = position[None, :] < doc_span[:, None]
    source = jnp.where(in_slot, first_row[:, None] + position[None, :], 0)
    outgoing = jnp.take(targets, source.reshape(-1), axis=0).reshape(
        loaders, slot_rows, feature_cols
    )
    arrived = lax.all_to_all(outgoing, DP, split_axis=0, concat_axis=0, tiled=True)
    my_lengths = lax.dynamic_index_in_dim(doc_lengths, device, 0, keepdims=False)
    my_owners = lax.dynamic_index_in_dim(doc_owners, device, 0, keepdims=False)
    my_starts = jnp.cumsum(my_lengths) - my_lengths
    token_pos = jnp.arange(tok_count, dtype=jnp.int32)
    inside = (token_pos[:, None] >= my_starts[None, :]) & (
        token_pos[:, None] < (my_starts + my_lengths)[None, :]
    )
    inside_int = inside.astype(jnp.int32)
    goal_index = (
        jnp.sum(inside_int * (my_owners * slot_rows - my_starts)[None, :], axis=1) + token_pos
    )
    weight = jnp.sum(
        inside.astype(jnp.float32) / my_lengths.astype(jnp.float32)[None, :], axis=1
    )
    picks = (
        jnp.arange(loaders * slot_rows, dtype=jnp.int32)[:, None] == goal_index[None, :]
    ).astype(jnp.bfloat16)
    goal_cols = lax.dot_general(
        arrived.reshape(loaders * slot_rows, feature_cols),
        picks,
        (((0,), (0,)), ((), ())),
        preferred_element_type=jnp.float32,
    ).astype(jnp.bfloat16)
    hess_first, mixed_rows = curvature(
        tokens,
        goal_cols,
        weight,
        first_blocks,
        second_factor_blocks,
        down_blocks,
        first_tangent,
        second_factor_tangent,
    )
    local_blocks = hess_first.shape[0]
    x_size = lax.axis_size("x")
    me_x = lax.axis_index("x")
    mixed_in = lax.all_to_all(
        mixed_rows.astype(jnp.bfloat16), "y", split_axis=0, concat_axis=0, tiled=True
    )
    first_part = (
        hess_first.reshape(local_blocks, loaders, -1)
        .transpose(1, 0, 2)
        .astype(jnp.bfloat16)
        .reshape(loaders // x_size, x_size, local_blocks, -1)
    )
    first_rows = lax.dynamic_index_in_dim(first_part, me_x, 1, keepdims=False).astype(
        jnp.float32
    )
    for shift in range(1, x_size):
        piece = lax.dynamic_index_in_dim(first_part, (me_x + shift) % x_size, 1, keepdims=False)
        moved = lax.ppermute(piece, "x", [(i, (i + shift) % x_size) for i in range(x_size)])
        first_rows = first_rows + moved.astype(jnp.float32)
    first_in = lax.all_to_all(
        first_rows.astype(jnp.bfloat16), "y", split_axis=0, concat_axis=0, tiled=True
    )
    hess_first = jnp.sum(first_in.astype(jnp.float32), axis=0).reshape(
        local_blocks, -1, first_blocks.shape[2]
    )
    hess_mixed = jnp.sum(mixed_in.astype(jnp.float32), axis=0).reshape(
        local_blocks, -1, second_factor_blocks.shape[2]
    )
    return (hess_first, hess_mixed)


def solution(mesh):
    dp_size, feat_size = mesh.shape["dp"], mesh.shape["feat"]
    x_size = 4
    view = Mesh(
        mesh.devices.reshape(dp_size // x_size, x_size, feat_size // 2, 2),
        ("y", "x", "z", "core"),
    )
    in_specs = (
        P(DP, FE),
        P(DP, FE),
        P(FE, None, None),
        P(FE, None, None),
        P(FE, None, None),
        P(FE, None, None),
        P(FE, None, None),
        P(),
        P(),
        P(),
    )
    out_specs = (P(FE, DP, None), P(FE, DP, None))
    return jax.shard_map(
        per_device, mesh=view, in_specs=in_specs, out_specs=out_specs, check_vma=False
    )
```

```python
import jax
import jax.numpy as jnp
from jax import lax
from jax.sharding import Mesh, PartitionSpec as P


DP = ("y", "x")
FE = ("z", "core")

inv_root_two = 0.7071067811865476
inv_root_two_pi = 0.3989422804014327


def curvature(
    tok_rows,
    goal_rows,
    weight,
    first_blocks,
    second_factor_blocks,
    down_blocks,
    first_tangent,
    second_factor_tangent,
):
    features = lax.axis_size(FE)
    row_count = tok_rows.shape[0]
    local_blocks, block_in, block_out = first_blocks.shape
    pair_size = block_out // (local_blocks * features)
    token_blocks = tok_rows.reshape(row_count, local_blocks, block_in)
    goal_blocks = goal_rows.reshape(local_blocks, block_in, row_count)
    split_shape = (local_blocks, block_in, features, local_blocks, pair_size)
    down_shape = (local_blocks, features, local_blocks, pair_size, block_in)
    first_act = jnp.einsum(
        "rki,kiGgc->Ggkcr",
        token_blocks,
        first_blocks.reshape(split_shape),
        preferred_element_type=jnp.float32,
    ).astype(jnp.bfloat16)
    tangents = jnp.einsum(
        "rki,kiGgc->Ggkcr",
        token_blocks,
        first_tangent.reshape(split_shape),
        preferred_element_type=jnp.float32,
    ).astype(jnp.bfloat16)
    out_grad = (
        jnp.einsum(
            "kdr,kGgcd->Ggkcr",
            goal_blocks,
            down_blocks.reshape(down_shape),
            preferred_element_type=jnp.float32,
        )
        * weight
    ).astype(jnp.bfloat16)
    merged = (features, local_blocks, local_blocks * pair_size, row_count)
    stacked = jnp.stack([first_act.reshape(merged), tangents.reshape(merged)], axis=1)
    mixed = lax.all_to_all(stacked, FE, split_axis=0, concat_axis=3, tiled=True)
    hidden = lax.all_to_all(out_grad.reshape(merged), FE, split_axis=0, concat_axis=2, tiled=True)
    hidden_shape = (local_blocks, block_out, row_count)
    mixed_activation = mixed[0, 0].reshape(hidden_shape)
    mixed_tangent_value = mixed[0, 1].reshape(hidden_shape)
    hidden_grad = hidden[0].reshape(hidden_shape)
    pre_act = jnp.einsum(
        "vca,vcf->vfa", mixed_activation, second_factor_blocks, preferred_element_type=jnp.float32
    )
    pre_tan = jnp.einsum(
        "vca,vcf->vfa",
        mixed_tangent_value,
        second_factor_blocks,
        preferred_element_type=jnp.float32,
    ) + jnp.einsum(
        "vca,vcf->vfa", mixed_activation, second_factor_tangent, preferred_element_type=jnp.float32
    )
    density = jnp.exp(-0.5 * pre_act * pre_act) * inv_root_two_pi
    normal_cdf = 0.5 * (1.0 + lax.erf(pre_act * inv_root_two))
    preactivation_gradient = (hidden_grad * (normal_cdf + pre_act * density)).astype(jnp.bfloat16)
    preactivation_tangent_gradient = (
        hidden_grad * (density * (2.0 - pre_act * pre_act)) * pre_tan
    ).astype(jnp.bfloat16)
    hess_mixed = jnp.einsum(
        "evp,eqp->evq",
        mixed_tangent_value,
        preactivation_gradient,
        preferred_element_type=jnp.float32,
    ) + jnp.einsum(
        "evp,eqp->evq",
        mixed_activation,
        preactivation_tangent_gradient,
        preferred_element_type=jnp.float32,
    )
    pos_shape = (local_blocks, features, local_blocks, pair_size, block_out)
    back_mixed = jnp.einsum(
        "bip,bFkci->Fkbcp",
        preactivation_tangent_gradient,
        second_factor_blocks.reshape(pos_shape),
        preferred_element_type=jnp.float32,
    ) + jnp.einsum(
        "bip,bFkci->Fkbcp",
        preactivation_gradient,
        second_factor_tangent.reshape(pos_shape),
        preferred_element_type=jnp.float32,
    )
    back_merged = back_mixed.astype(jnp.bfloat16).reshape(
        features, local_blocks, local_blocks * pair_size, row_count
    )
    loaders = lax.axis_size(DP)
    x_size = lax.axis_size("x")
    me_x = lax.axis_index("x")
    mixed_part = (
        hess_mixed.reshape(local_blocks, loaders, -1)
        .transpose(1, 0, 2)
        .astype(jnp.bfloat16)
        .reshape(loaders // x_size, x_size, local_blocks, -1)
    )
    mixed_rows = lax.dynamic_index_in_dim(mixed_part, me_x, 1, keepdims=False).astype(
        jnp.float32
    )
    for shift in range(1, x_size):
        piece = lax.dynamic_index_in_dim(mixed_part, (me_x + shift) % x_size, 1, keepdims=False)
        moved = lax.ppermute(piece, "x", [(i, (i + shift) % x_size) for i in range(x_size)])
        mixed_rows = mixed_rows + moved.astype(jnp.float32)
    back_first = lax.all_to_all(back_merged, FE, split_axis=0, concat_axis=2, tiled=True)
    back_first = back_first.reshape(local_blocks, block_out, row_count)
    hess_first = jnp.einsum(
        "rki,kjr->kij", token_blocks, back_first, preferred_element_type=jnp.float32
    )
    return (hess_first, mixed_rows)


def per_device(
    tokens,
    targets,
    first_blocks,
    second_factor_blocks,
    down_blocks,
    first_tangent,
    second_factor_tangent,
    doc_lengths,
    doc_owners,
    pack_offsets,
):
    loaders = lax.axis_size(DP)
    device = lax.axis_index(DP)
    tok_count = tokens.shape[0]
    feature_cols = tokens.shape[1]
    slot_rows = 2 * tok_count // loaders
    position = jnp.arange(slot_rows, dtype=jnp.int32)
    mine = (doc_owners == device).astype(jnp.int32)
    first_row = jnp.sum(mine * pack_offsets, axis=1)
    doc_span = jnp.sum(mine * doc_lengths, axis=1)
    in_slot = position[None, :] < doc_span[:, None]
    source = jnp.where(in_slot, first_row[:, None] + position[None, :], 0)
    outgoing = jnp.take(targets, source.reshape(-1), axis=0).reshape(
        loaders, slot_rows, feature_cols
    )
    x_size = lax.axis_size("x")
    y_size = loaders // x_size
    me_x = lax.axis_index("x")
    me_y = lax.axis_index("y")
    by_column = outgoing.reshape(y_size, x_size, slot_rows, feature_cols).transpose(1, 0, 2, 3)
    got = [lax.dynamic_index_in_dim(by_column, me_x, 0, keepdims=False)]
    for shift in range(1, x_size):
        piece = lax.dynamic_index_in_dim(by_column, (me_x + shift) % x_size, 0, keepdims=False)
        got.append(lax.ppermute(piece, "x", [(i, (i + shift) % x_size) for i in range(x_size)]))
    from_x = jnp.take(jnp.stack(got), (me_x - jnp.arange(x_size)) % x_size, axis=0)
    by_row = from_x.transpose(1, 0, 2, 3)
    got = [lax.dynamic_index_in_dim(by_row, me_y, 0, keepdims=False)]
    for shift in range(1, y_size):
        piece = lax.dynamic_index_in_dim(by_row, (me_y + shift) % y_size, 0, keepdims=False)
        got.append(lax.ppermute(piece, "y", [(i, (i + shift) % y_size) for i in range(y_size)]))
    arrived = jnp.take(jnp.stack(got), (me_y - jnp.arange(y_size)) % y_size, axis=0)
    my_lengths = lax.dynamic_index_in_dim(doc_lengths, device, 0, keepdims=False)
    my_owners = lax.dynamic_index_in_dim(doc_owners, device, 0, keepdims=False)
    my_starts = jnp.cumsum(my_lengths) - my_lengths
    token_pos = jnp.arange(tok_count, dtype=jnp.int32)
    inside = (token_pos[:, None] >= my_starts[None, :]) & (
        token_pos[:, None] < (my_starts + my_lengths)[None, :]
    )
    inside_int = inside.astype(jnp.int32)
    goal_index = (
        jnp.sum(inside_int * (my_owners * slot_rows - my_starts)[None, :], axis=1) + token_pos
    )
    weight = jnp.sum(
        inside.astype(jnp.float32) / my_lengths.astype(jnp.float32)[None, :], axis=1
    )
    picks = (
        jnp.arange(loaders * slot_rows, dtype=jnp.int32)[:, None] == goal_index[None, :]
    ).astype(jnp.bfloat16)
    goal_cols = lax.dot_general(
        arrived.reshape(loaders * slot_rows, feature_cols),
        picks,
        (((0,), (0,)), ((), ())),
        preferred_element_type=jnp.float32,
    ).astype(jnp.bfloat16)
    hess_first, mixed_rows = curvature(
        tokens,
        goal_cols,
        weight,
        first_blocks,
        second_factor_blocks,
        down_blocks,
        first_tangent,
        second_factor_tangent,
    )
    local_blocks = hess_first.shape[0]
    x_size = lax.axis_size("x")
    first_part = (
        hess_first.reshape(local_blocks, loaders, -1)
        .transpose(1, 0, 2)
        .astype(jnp.bfloat16)
        .reshape(loaders // x_size, x_size, local_blocks, -1)
    )
    first_width = first_part.shape[3]
    across_x = lax.all_to_all(first_part, "x", split_axis=1, concat_axis=1, tiled=True)
    first_rows = jnp.sum(across_x.astype(jnp.float32), axis=1)
    row_sums = jnp.concatenate([first_rows, mixed_rows], axis=2).astype(jnp.bfloat16)
    across_y = lax.all_to_all(row_sums, "y", split_axis=0, concat_axis=0, tiled=True)
    total = jnp.sum(across_y.astype(jnp.float32), axis=0)
    hess_first = total[:, :first_width].reshape(local_blocks, -1, first_blocks.shape[2])
    hess_mixed = total[:, first_width:].reshape(local_blocks, -1, second_factor_blocks.shape[2])
    return (hess_first, hess_mixed)


def solution(mesh):
    dp_size, feat_size = mesh.shape["dp"], mesh.shape["feat"]
    x_size = 4
    view = Mesh(
        mesh.devices.reshape(dp_size // x_size, x_size, feat_size // 2, 2),
        ("y", "x", "z", "core"),
    )
    in_specs = (
        P(DP, FE),
        P(DP, FE),
        P(FE, None, None),
        P(FE, None, None),
        P(FE, None, None),
        P(FE, None, None),
        P(FE, None, None),
        P(),
        P(),
        P(),
    )
    out_specs = (P(FE, DP, None), P(FE, DP, None))

    return jax.shard_map(per_device, mesh=view, in_specs=in_specs, out_specs=out_specs, check_vma=False)
```

```python
import jax
import jax.numpy as jnp
from jax import lax
from jax.sharding import Mesh, PartitionSpec as P

DP = ("y", "x")
FE = ("z", "core")

inv_root_two = 0.7071067811865476
inv_root_two_pi = 0.3989422804014327


def curvature(
    tok_rows,
    goal_rows,
    weight,
    first_blocks,
    second_factor_blocks,
    down_blocks,
    first_tangent,
    second_factor_tangent,
):
    features = lax.axis_size(FE)
    row_count = tok_rows.shape[0]
    local_blocks, block_in, block_out = first_blocks.shape
    pair_size = block_out // (local_blocks * features)
    token_blocks = tok_rows.reshape(row_count, local_blocks, block_in)
    goal_blocks = goal_rows.reshape(local_blocks, block_in, row_count)
    split_shape = (local_blocks, block_in, features, local_blocks, pair_size)
    down_shape = (local_blocks, features, local_blocks, pair_size, block_in)
    first_act = jnp.einsum(
        "rki,kiGgc->Ggkcr",
        token_blocks,
        first_blocks.reshape(split_shape),
        preferred_element_type=jnp.float32,
    ).astype(jnp.bfloat16)
    tangents = jnp.einsum(
        "rki,kiGgc->Ggkcr",
        token_blocks,
        first_tangent.reshape(split_shape),
        preferred_element_type=jnp.float32,
    ).astype(jnp.bfloat16)
    out_grad = (
        jnp.einsum(
            "kdr,kGgcd->Ggkcr",
            goal_blocks,
            down_blocks.reshape(down_shape),
            preferred_element_type=jnp.float32,
        )
        * weight
    ).astype(jnp.bfloat16)
    merged = (features, local_blocks, local_blocks * pair_size, row_count)
    stacked = jnp.stack(
        [first_act.reshape(merged), tangents.reshape(merged), out_grad.reshape(merged)], axis=1
    )
    mixed = lax.all_to_all(stacked, FE, split_axis=0, concat_axis=3, tiled=True)
    hidden_shape = (local_blocks, block_out, row_count)
    mixed_activation = mixed[0, 0].reshape(hidden_shape)
    mixed_tangent_value = mixed[0, 1].reshape(hidden_shape)
    hidden_grad = mixed[0, 2].reshape(hidden_shape)
    pre_act = jnp.einsum(
        "vca,vcf->vfa", mixed_activation, second_factor_blocks, preferred_element_type=jnp.float32
    )
    pre_tan = jnp.einsum(
        "vca,vcf->vfa",
        mixed_tangent_value,
        second_factor_blocks,
        preferred_element_type=jnp.float32,
    ) + jnp.einsum(
        "vca,vcf->vfa", mixed_activation, second_factor_tangent, preferred_element_type=jnp.float32
    )
    density = jnp.exp(-0.5 * pre_act * pre_act) * inv_root_two_pi
    normal_cdf = 0.5 * (1.0 + lax.erf(pre_act * inv_root_two))
    preactivation_gradient = (hidden_grad * (normal_cdf + pre_act * density)).astype(jnp.bfloat16)
    preactivation_tangent_gradient = (
        hidden_grad * (density * (2.0 - pre_act * pre_act)) * pre_tan
    ).astype(jnp.bfloat16)
    hess_mixed = jnp.einsum(
        "evp,eqp->evq",
        mixed_tangent_value,
        preactivation_gradient,
        preferred_element_type=jnp.float32,
    ) + jnp.einsum(
        "evp,eqp->evq",
        mixed_activation,
        preactivation_tangent_gradient,
        preferred_element_type=jnp.float32,
    )
    pos_shape = (local_blocks, features, local_blocks, pair_size, block_out)
    back_mixed = jnp.einsum(
        "bip,bFkci->Fkbcp",
        preactivation_tangent_gradient,
        second_factor_blocks.reshape(pos_shape),
        preferred_element_type=jnp.float32,
    ) + jnp.einsum(
        "bip,bFkci->Fkbcp",
        preactivation_gradient,
        second_factor_tangent.reshape(pos_shape),
        preferred_element_type=jnp.float32,
    )
    back_merged = back_mixed.astype(jnp.bfloat16).reshape(
        features, local_blocks, local_blocks * pair_size, row_count
    )
    loaders = lax.axis_size(DP)
    x_size = lax.axis_size("x")
    me_x = lax.axis_index("x")
    mixed_part = (
        hess_mixed.reshape(local_blocks, loaders, -1)
        .transpose(1, 0, 2)
        .astype(jnp.bfloat16)
        .reshape(loaders // x_size, x_size, local_blocks, -1)
    )
    mixed_rows = lax.dynamic_index_in_dim(mixed_part, me_x, 1, keepdims=False).astype(
        jnp.float32
    )
    for shift in range(1, x_size):
        piece = lax.dynamic_index_in_dim(mixed_part, (me_x + shift) % x_size, 1, keepdims=False)
        moved = lax.ppermute(piece, "x", [(i, (i + shift) % x_size) for i in range(x_size)])
        mixed_rows = mixed_rows + moved.astype(jnp.float32)
    back_first = lax.all_to_all(back_merged, FE, split_axis=0, concat_axis=2, tiled=True)
    back_first = back_first.reshape(local_blocks, block_out, row_count)
    hess_first = jnp.einsum(
        "rki,kjr->kij", token_blocks, back_first, preferred_element_type=jnp.float32
    )
    return (hess_first, mixed_rows)


def per_device(
    tokens,
    targets,
    first_blocks,
    second_factor_blocks,
    down_blocks,
    first_tangent,
    second_factor_tangent,
    doc_lengths,
    doc_owners,
    pack_offsets,
):
    loaders = lax.axis_size(DP)
    device = lax.axis_index(DP)
    tok_count = tokens.shape[0]
    feature_cols = tokens.shape[1]
    slot_rows = 2 * tok_count // loaders
    position = jnp.arange(slot_rows, dtype=jnp.int32)
    mine = (doc_owners == device).astype(jnp.int32)
    first_row = jnp.sum(mine * pack_offsets, axis=1)
    doc_span = jnp.sum(mine * doc_lengths, axis=1)
    in_slot = position[None, :] < doc_span[:, None]
    source = jnp.where(in_slot, first_row[:, None] + position[None, :], 0)
    outgoing = targets.at[source.reshape(-1)].get(mode="promise_in_bounds").reshape(
        loaders, slot_rows, feature_cols
    )
    arrived = lax.all_to_all(outgoing, DP, split_axis=0, concat_axis=0, tiled=True)
    my_lengths = lax.dynamic_index_in_dim(doc_lengths, device, 0, keepdims=False)
    my_owners = lax.dynamic_index_in_dim(doc_owners, device, 0, keepdims=False)
    my_starts = jnp.cumsum(my_lengths) - my_lengths
    token_pos = jnp.arange(tok_count, dtype=jnp.int32)
    inside = (token_pos[:, None] >= my_starts[None, :]) & (
        token_pos[:, None] < (my_starts + my_lengths)[None, :]
    )
    inside_int = inside.astype(jnp.int32)
    goal_index = (
        jnp.sum(inside_int * (my_owners * slot_rows - my_starts)[None, :], axis=1) + token_pos
    )
    weight = jnp.sum(
        inside.astype(jnp.float32) / my_lengths.astype(jnp.float32)[None, :], axis=1
    )
    picks = (
        jnp.arange(loaders * slot_rows, dtype=jnp.int32)[:, None] == goal_index[None, :]
    ).astype(jnp.bfloat16)
    goal_cols = lax.dot_general(
        arrived.reshape(loaders * slot_rows, feature_cols),
        picks,
        (((0,), (0,)), ((), ())),
        preferred_element_type=jnp.float32,
    ).astype(jnp.bfloat16)
    hess_first, mixed_rows = curvature(
        tokens,
        goal_cols,
        weight,
        first_blocks,
        second_factor_blocks,
        down_blocks,
        first_tangent,
        second_factor_tangent,
    )
    local_blocks = hess_first.shape[0]
    x_size = lax.axis_size("x")
    first_part = (
        hess_first.reshape(local_blocks, loaders, -1)
        .transpose(1, 0, 2)
        .astype(jnp.bfloat16)
        .reshape(loaders // x_size, x_size, local_blocks, -1)
    )
    first_width = first_part.shape[3]
    across_x = lax.all_to_all(first_part, "x", split_axis=1, concat_axis=1, tiled=True)
    first_rows = jnp.sum(across_x.astype(jnp.float32), axis=1)
    row_sums = jnp.concatenate([first_rows, mixed_rows], axis=2).astype(jnp.bfloat16)
    across_y = lax.all_to_all(row_sums, "y", split_axis=0, concat_axis=0, tiled=True)
    total = jnp.sum(across_y.astype(jnp.float32), axis=0)
    hess_first = total[:, :first_width].reshape(local_blocks, -1, first_blocks.shape[2])
    hess_mixed = total[:, first_width:].reshape(local_blocks, -1, second_factor_blocks.shape[2])
    return (hess_first, hess_mixed)


def solution(mesh):
    dp_size, feat_size = mesh.shape["dp"], mesh.shape["feat"]
    x_size = 4
    view = Mesh(
        mesh.devices.reshape(dp_size // x_size, x_size, feat_size // 2, 2),
        ("y", "x", "z", "core"),
    )
    in_specs = (
        P(DP, FE),
        P(DP, FE),
        P(FE, None, None),
        P(FE, None, None),
        P(FE, None, None),
        P(FE, None, None),
        P(FE, None, None),
        P(),
        P(),
        P(),
    )
    out_specs = (P(FE, DP, None), P(FE, DP, None))
    return jax.shard_map(
        per_device, mesh=view, in_specs=in_specs, out_specs=out_specs, check_vma=False
    )
```
